32 devices in a mesh: groups: 2 (over x), seq: 16 (over z, y, core).
Axes of the slice: x: 2, y: 2, z: 4, core: 2. Of those that a mesh axis runs over, the one named last changes fastest.
Arguments:
- layer_input: bfloat16 [4096, 768], P(('groups', 'seq')), parts along dimension 0, may hold values from -60 to 60
- norm_gain: bfloat16 [768], replicated, may hold values from 0.099609375 to 1.8984375
- projection: bfloat16 [768, 2304], replicated, may hold values from -8 to 8
- output_weight: bfloat16 [768, 768], replicated, may hold values from -0.21875 to 0.21875
- deep_weight: bfloat16 [768, 512], replicated, may hold values from -0.21875 to 0.21875
- skip_weight: bfloat16 [768, 512], replicated, may hold values from -0.21875 to 0.21875
- conv_kernel: bfloat16 [3, 3, 3, 128, 64], replicated, may hold values from -0.109375 to 0.109375
Outputs:
- encoded: bfloat16 [4096, 768], P(('groups', 'seq')), parts along dimension 0
- decoded: bfloat16 [32, 2, 32, 16, 64], P(('groups', 'seq')), parts along dimension 0
The draws below stay inside these ranges and needn't reach their ends.
There are 2 independent parts, one for each index of `groups`. The reference program is written for one: setup_inputs(seed, part) draws one part's arguments, and reference() takes and returns one part's arrays. A program takes and returns all parts, laid end to end along the dimension named above; an argument that names none is the same for every part. Nothing has to cross between parts.
All inputs are finite; a program needn't handle non-finite values.
Results may differ from the reference program's by a relative error of at most 0.0078.
Values may be sent and summed in bfloat16 or wider, within the bound.
No kernel may reach another device: no remote copies, remote signals or barrier semaphores. Data moves between devices by JAX's collectives and lax.ppermute only.
A program may use at most 128 MiB of HBM per device.

```python
import math
import jax
import jax.numpy as jnp
from jax import lax

D = 768
HEADS = 12
CH = 64
GZ = 8
GY = 32
GX = 8
TOKENS = 2048
XV = 16
YV = 64
ZV = 16
BLOCKS = 16


def draw_layer_input(key, part):
    key_base = jax.random.fold_in(key, 0)
    base = jax.random.normal(key_base, (TOKENS, D), jnp.float32)
    return jnp.clip(base, -60.0, 60.0).astype(jnp.bfloat16)


def draw_projection(key, part):
    key_base = jax.random.fold_in(key, 0)
    base = jax.random.normal(key_base, (D, 3 * D), jnp.float32) / math.sqrt(D)
    factor = jnp.where(jnp.arange(3 * D)[None, :] < 2 * D, 2.0, 1.0)
    return jnp.clip(base * factor, -8.0, 8.0).astype(jnp.bfloat16)


def gaussian(rng, shape, scale, most, dtype=jnp.bfloat16):
    array = scale * jax.random.normal(rng, shape, jnp.float32)
    return jnp.clip(array, min=-most, max=most).astype(dtype)


def setup_inputs(seed: int = 0, part: int = 0) -> dict:
    keys = jax.random.split(jax.random.key(seed), 8)
    part_splits = jax.random.split(jax.random.fold_in(keys[7], part), 8)
    return {
        "layer_input": draw_layer_input(jax.random.fold_in(jax.random.fold_in(keys[7], part), 71), part),
        "norm_gain": jnp.clip(1.0 + 0.18 * jax.random.normal(keys[1], (D,), jnp.float32), 0.099609375, 1.8984375).astype(jnp.bfloat16),
        "projection": draw_projection(jax.random.fold_in(keys[7], 71), part),
        "output_weight": gaussian(keys[3], (D, D), D ** -0.5, 0.21875),
        "deep_weight": gaussian(keys[4], (D, 8 * CH), D ** -0.5, 0.21875),
        "skip_weight": gaussian(keys[5], (D, 8 * CH), D ** -0.5, 0.21875),
        "conv_kernel": gaussian(keys[6], (3, 3, 3, 2 * CH, CH), (54 * CH) ** -0.5, 0.109375),
    }


epsilon = 1e-06
leak_slope = 0.01

def layer_norm(inputs, gain):
    values32 = inputs.astype(jnp.float32)
    row_mean = lax.optimization_barrier(jnp.mean(values32, axis=-1, keepdims=True))
    centered = values32 - row_mean
    row_var = lax.optimization_barrier(jnp.mean(centered * centered, axis=-1, keepdims=True))
    return centered * lax.rsqrt(row_var + epsilon) * gain.astype(jnp.float32)

def to_voxels(flat_out, channels):
    extent_x, extent_y, extent_z = (flat_out.shape[0], flat_out.shape[1], flat_out.shape[2])
    shaped = flat_out.reshape(extent_x, extent_y, extent_z, 2, 2, 2, channels)
    shaped = shaped.transpose(0, 3, 1, 4, 2, 5, 6)
    return shaped.reshape(2 * extent_x, 2 * extent_y, 2 * extent_z, channels)

def upsample(token_grid, weight):
    model_width = token_grid.shape[-1]
    product = jnp.dot(token_grid.reshape(-1, model_width), weight, preferred_element_type=jnp.float32)
    flat_out = product.astype(jnp.bfloat16).reshape(token_grid.shape[:3] + (weight.shape[1],))
    return to_voxels(flat_out, weight.shape[1] // 8)

def reference(layer_input, norm_gain, projection, output_weight, deep_weight, skip_weight, conv_kernel):
    head_size = D // HEADS
    score_scale = 1.0 / math.sqrt(head_size)
    normed = layer_norm(layer_input, norm_gain).astype(jnp.bfloat16)
    projected = jnp.dot(normed, projection, preferred_element_type=jnp.float32).astype(jnp.bfloat16)
    queries = projected[:, :D].reshape(TOKENS, HEADS, head_size)
    key_rows = projected[:, D:2 * D].reshape(TOKENS, HEADS, head_size).astype(jnp.float32)
    value_rows = projected[:, 2 * D:].reshape(TOKENS, HEADS, head_size).astype(jnp.float32)
    block_size = math.gcd(512, TOKENS)

    def attend_block(query_block):
        scores = jnp.einsum('qhd,khd->hqk', query_block.astype(jnp.float32), key_rows) * score_scale
        row_max = lax.optimization_barrier(jnp.max(scores, axis=-1, keepdims=True))
        exp_scores = jnp.exp(scores - row_max)
        denominator = lax.optimization_barrier(jnp.sum(exp_scores, axis=-1))
        rounded = lax.optimization_barrier(exp_scores.astype(jnp.bfloat16))
        numerator = jnp.einsum('hqk,khd->qhd', rounded.astype(jnp.float32), value_rows)
        return (numerator / denominator.T[:, :, None]).astype(jnp.bfloat16)
    blocks = queries.reshape(TOKENS // block_size, block_size, HEADS, head_size)
    attended = lax.map(attend_block, blocks).reshape(TOKENS, D)
    encoded = (layer_input.astype(jnp.float32) + jnp.dot(attended, output_weight, preferred_element_type=jnp.float32)).astype(jnp.bfloat16)
    input_grid = layer_input.reshape(GX, GY, GZ, D)
    encoded_grid = encoded.reshape(GX, GY, GZ, D)
    joined = jnp.concatenate([upsample(encoded_grid, deep_weight), upsample(input_grid, skip_weight)], axis=-1)
    padded = jnp.pad(joined, ((1, 1), (1, 1), (1, 1), (0, 0)))
    accumulated = jnp.zeros((XV * YV * ZV, CH), jnp.float32)
    for tap_x in range(3):
        for tap_y in range(3):
            for tap_z in range(3):
                window = padded[tap_x:tap_x + XV, tap_y:tap_y + YV, tap_z:tap_z + ZV, :].reshape(-1, 2 * CH)
                accumulated = accumulated + jnp.dot(window, conv_kernel[tap_x, tap_y, tap_z], preferred_element_type=jnp.float32)
    field = jnp.where(accumulated > 0, accumulated, leak_slope * accumulated).astype(jnp.bfloat16).reshape(XV, YV, ZV, CH)
    decoded = field.reshape(GX, 2, 2, YV // 2, ZV, CH).transpose(0, 2, 1, 3, 4, 5).reshape(BLOCKS, 2, YV // 2, ZV, CH)
    return (encoded, decoded)
```

```python
import math

import jax
import jax.numpy as jnp
from jax import lax
from jax.experimental import pallas as pl
from jax.sharding import PartitionSpec as P

HEADS = 12
GZ = 8


epsilon = 1e-06
leak_slope = 0.01


def shifted(block, axis, distance):
    devices = range(lax.axis_size(axis))
    route = [(i - distance, i) for i in devices if i - distance in devices]
    return lax.ppermute(block, axis, route)


def swapped(x, axis, distance):
    return lax.ppermute(x, axis, [(i, i ^ 1 << distance) for i in range(lax.axis_size(axis))])


def layer_norm(inputs, gain):
    values32 = inputs.astype(jnp.float32)
    row_mean = jnp.mean(values32, axis=-1, keepdims=True)
    centered = values32 - row_mean
    row_var = jnp.mean(centered * centered, axis=-1, keepdims=True)
    return centered * lax.rsqrt(row_var + epsilon) * gain.astype(jnp.float32)


def to_voxels(flat_out, channels):
    extent_x, extent_y, extent_z = (flat_out.shape[0], flat_out.shape[1], flat_out.shape[2])
    shaped = flat_out.reshape(extent_x, extent_y, extent_z, 2, 2, 2, channels)
    shaped = shaped.transpose(0, 3, 1, 4, 2, 5, 6)
    return shaped.reshape(2 * extent_x, 2 * extent_y, 2 * extent_z, channels)


def upsample(token_grid, weight):
    model_width = token_grid.shape[-1]
    product = jnp.dot(
        token_grid.reshape(-1, model_width), weight, preferred_element_type=jnp.float32
    )
    flat_out = product.astype(jnp.bfloat16).reshape(token_grid.shape[:3] + (weight.shape[1],))
    return to_voxels(flat_out, weight.shape[1] // 8)


def convolve(full_xy, conv_kernel):
    accumulated = lax.conv_general_dilated(
        full_xy[None],
        conv_kernel,
        window_strides=(1, 1, 1),
        padding=((0, 0), (0, 0), (1, 1)),
        dimension_numbers=("NDHWC", "DHWIO", "NDHWC"),
        preferred_element_type=jnp.float32,
    )[0]
    activated = jnp.where(accumulated > 0, accumulated, leak_slope * accumulated)
    return activated.astype(jnp.bfloat16)


def plane_send(plane, offset):
    return shifted(plane, "seq", offset)


def attention_kernel(q_ref, k_ref, v_ref, o_ref, *, head_size, score_scale):
    pair = q_ref.shape[-1]
    lane = lax.broadcasted_iota(jnp.int32, (1, pair), 1)
    q = q_ref[...]
    k = k_ref[...]
    v = v_ref[...]
    result = None
    for h in range(pair // head_size):
        in_head = (lane >= h * head_size) & (lane < (h + 1) * head_size)
        q_h = jnp.where(in_head, q, jnp.zeros_like(q))
        scores = (
            lax.dot_general(q_h, k, (((1,), (1,)), ((), ())), preferred_element_type=jnp.float32)
            * score_scale
        )
        row_max = jnp.max(scores, axis=-1, keepdims=True)
        exp_scores = jnp.exp(scores - row_max)
        denominator = jnp.sum(exp_scores, axis=-1, keepdims=True)
        numerator = jnp.dot(
            exp_scores.astype(jnp.bfloat16), v, preferred_element_type=jnp.float32
        )
        head_out = numerator / denominator
        result = head_out if result is None else jnp.where(in_head, head_out, result)
    o_ref[...] = result.astype(o_ref.dtype)


def attention(queries, key_value, head_size, score_scale):
    token_count, model_width = queries.shape
    total = key_value.shape[0]
    pair = 2 * head_size
    pairs = model_width // pair
    kernel = lambda *refs: attention_kernel(*refs, head_size=head_size, score_scale=score_scale)
    return pl.pallas_call(
        kernel,
        grid=(pairs,),
        in_specs=[
            pl.BlockSpec((token_count, pair), lambda j: (0, j)),
            pl.BlockSpec((total, pair), lambda j: (0, j)),
            pl.BlockSpec((total, pair), lambda j: (0, j + pairs)),
        ],
        out_specs=pl.BlockSpec((token_count, pair), lambda j: (0, j)),
        out_shape=jax.ShapeDtypeStruct((token_count, model_width), jnp.bfloat16),
    )(queries, key_value, key_value)


def body(layer_input, norm_gain, projection, output_weight, deep_weight, skip_weight, conv_kernel):
    token_count, model_width = layer_input.shape
    head_size = model_width // HEADS
    score_scale = 1.0 / math.sqrt(head_size)
    all_input = lax.all_gather(layer_input, "seq", axis=0, tiled=True)
    normed = layer_norm(layer_input, norm_gain).astype(jnp.bfloat16)
    queries = jnp.dot(
        normed, projection[:, :model_width], preferred_element_type=jnp.float32
    ).astype(jnp.bfloat16)
    all_normed = layer_norm(all_input, norm_gain).astype(jnp.bfloat16)
    key_value = jnp.dot(
        all_normed, projection[:, model_width:], preferred_element_type=jnp.float32
    ).astype(jnp.bfloat16)
    attended = attention(queries, key_value, head_size, score_scale)
    encoded = (
        layer_input.astype(jnp.float32)
        + jnp.dot(attended, output_weight, preferred_element_type=jnp.float32)
    ).astype(jnp.bfloat16)
    position = lax.axis_index("seq")
    half_rows = token_count // GZ
    input_grid = layer_input.reshape(1, half_rows, GZ, model_width)
    encoded_grid = encoded.reshape(1, half_rows, GZ, model_width)
    joined = jnp.concatenate(
        [upsample(encoded_grid, deep_weight), upsample(input_grid, skip_weight)], axis=-1
    )
    lower_half = position % 2 == 0
    boundary = jnp.where(lower_half, joined[:, -1:], joined[:, :1])
    partner = swapped(boundary, "seq", 0)
    zero_plane = jnp.zeros_like(partner)
    low_rim = jnp.where(lower_half, zero_plane, partner)
    high_rim = jnp.where(lower_half, partner, zero_plane)
    extended = jnp.concatenate([low_rim, joined, high_rim], axis=1)
    full_xy = jnp.concatenate(
        [plane_send(extended[-1:], 2), extended, plane_send(extended[:1], -2)], axis=0
    )
    decoded = convolve(full_xy, conv_kernel)[None]
    return (encoded, decoded)


def solution(mesh):
    return jax.shard_map(
        body,
        mesh=mesh,
        in_specs=(P(("groups", "seq"), None), P(), P(), P(), P(), P(), P()),
        out_specs=(P(("groups", "seq"), None), P(("groups", "seq"), None, None, None, None)),
        check_vma=False,
    )
```

```python
import math

import jax
import jax.numpy as jnp
from jax import lax
from jax.experimental import pallas as pl
from jax.sharding import PartitionSpec as P

HEADS = 12
GZ = 8


epsilon = 1e-06
leak_slope = 0.01


def shifted(block, axis, distance):
    devices = range(lax.axis_size(axis))
    route = [(i - distance, i) for i in devices if i - distance in devices]
    return lax.ppermute(block, axis, route)


def swapped(x, axis, distance):
    return lax.ppermute(x, axis, [(i, i ^ 1 << distance) for i in range(lax.axis_size(axis))])


def layer_norm(inputs, gain):
    values32 = inputs.astype(jnp.float32)
    row_mean = jnp.mean(values32, axis=-1, keepdims=True)
    centered = values32 - row_mean
    row_var = jnp.mean(centered * centered, axis=-1, keepdims=True)
    return centered * lax.rsqrt(row_var + epsilon) * gain.astype(jnp.float32)


def to_voxels(flat_out, channels):
    extent_x, extent_y, extent_z = (flat_out.shape[0], flat_out.shape[1], flat_out.shape[2])
    shaped = flat_out.reshape(extent_x, extent_y, extent_z, 2, 2, 2, channels)
    shaped = shaped.transpose(0, 3, 1, 4, 2, 5, 6)
    return shaped.reshape(2 * extent_x, 2 * extent_y, 2 * extent_z, channels)


def upsample(token_grid, weight):
    model_width = token_grid.shape[-1]
    product = jnp.dot(
        token_grid.reshape(-1, model_width), weight, preferred_element_type=jnp.float32
    )
    flat_out = product.astype(jnp.bfloat16).reshape(token_grid.shape[:3] + (weight.shape[1],))
    return to_voxels(flat_out, weight.shape[1] // 8)


def convolve(full_xy, conv_kernel):
    accumulated = lax.conv_general_dilated(
        full_xy[None],
        conv_kernel,
        window_strides=(1, 1, 1),
        padding=((0, 0), (0, 0), (1, 1)),
        dimension_numbers=("NDHWC", "DHWIO", "NDHWC"),
        preferred_element_type=jnp.float32,
    )[0]
    activated = jnp.where(accumulated > 0, accumulated, leak_slope * accumulated)
    return activated.astype(jnp.bfloat16)


def plane_send(plane, offset):
    return shifted(plane, "seq", offset)


def attention_kernel(*refs, head_size, score_scale, chunks):
    q_ref = refs[0]
    k_refs = refs[1 : 1 + chunks]
    v_refs = refs[1 + chunks : 1 + 2 * chunks]
    o_ref = refs[-1]
    pair = q_ref.shape[-1]
    lane = lax.broadcasted_iota(jnp.int32, (1, pair), 1)
    q = q_ref[...]
    result = None
    for h in range(pair // head_size):
        in_head = (lane >= h * head_size) & (lane < (h + 1) * head_size)
        q_h = jnp.where(in_head, q, jnp.zeros_like(q))
        scores = [
            lax.dot_general(
                q_h, k_ref[...], (((1,), (1,)), ((), ())), preferred_element_type=jnp.float32
            )
            * score_scale
            for k_ref in k_refs
        ]
        row_max = scores[0].max(axis=-1, keepdims=True)
        for block in scores[1:]:
            row_max = jnp.maximum(row_max, block.max(axis=-1, keepdims=True))
        denominator = None
        numerator = None
        for block, v_ref in zip(scores, v_refs):
            exp_scores = jnp.exp(block - row_max)
            part_sum = jnp.sum(exp_scores, axis=-1, keepdims=True)
            part = jnp.dot(
                exp_scores.astype(jnp.bfloat16), v_ref[...], preferred_element_type=jnp.float32
            )
            denominator = part_sum if denominator is None else denominator + part_sum
            numerator = part if numerator is None else numerator + part
        head_out = numerator / denominator
        result = head_out if result is None else jnp.where(in_head, head_out, result)
    o_ref[...] = result.astype(o_ref.dtype)


def attention(queries, kv_chunks, head_size, score_scale):
    token_count, model_width = queries.shape
    pair = 2 * head_size
    pairs = model_width // pair
    chunks = len(kv_chunks)
    kernel = lambda *refs: attention_kernel(
        *refs, head_size=head_size, score_scale=score_scale, chunks=chunks
    )
    key_specs = [pl.BlockSpec((c.shape[0], pair), lambda j: (0, j)) for c in kv_chunks]
    value_specs = [pl.BlockSpec((c.shape[0], pair), lambda j: (0, j + pairs)) for c in kv_chunks]
    return pl.pallas_call(
        kernel,
        grid=(pairs,),
        in_specs=[pl.BlockSpec((token_count, pair), lambda j: (0, j))] + key_specs + value_specs,
        out_specs=pl.BlockSpec((token_count, pair), lambda j: (0, j)),
        out_shape=jax.ShapeDtypeStruct((token_count, model_width), jnp.bfloat16),
    )(queries, *kv_chunks, *kv_chunks)


def gathered_rows(rows):
    devices = lax.axis_size("seq")
    local = [rows]
    for distance in range(2, devices, 2):
        local.append(lax.ppermute(rows, "seq", [(i, (i + distance) % devices) for i in range(devices)]))
    partner = [lax.ppermute(c, "seq", [(i, i ^ 1) for i in range(devices)]) for c in local]
    return local + partner


def body(layer_input, norm_gain, projection, output_weight, deep_weight, skip_weight, conv_kernel):
    token_count, model_width = layer_input.shape
    head_size = model_width // HEADS
    score_scale = 1.0 / math.sqrt(head_size)
    chunks = gathered_rows(layer_input)
    normed = layer_norm(layer_input, norm_gain).astype(jnp.bfloat16)
    queries = jnp.dot(
        normed, projection[:, :model_width], preferred_element_type=jnp.float32
    ).astype(jnp.bfloat16)
    kv_weight = projection[:, model_width:]
    kv_chunks = [jnp.dot(normed, kv_weight, preferred_element_type=jnp.float32).astype(jnp.bfloat16)]
    for chunk in chunks[1:]:
        chunk_normed = layer_norm(chunk, norm_gain).astype(jnp.bfloat16)
        kv_chunks.append(
            jnp.dot(chunk_normed, kv_weight, preferred_element_type=jnp.float32).astype(jnp.bfloat16)
        )
    attended = attention(queries, kv_chunks, head_size, score_scale)
    encoded = (
        layer_input.astype(jnp.float32)
        + jnp.dot(attended, output_weight, preferred_element_type=jnp.float32)
    ).astype(jnp.bfloat16)
    position = lax.axis_index("seq")
    half_rows = token_count // GZ
    input_grid = layer_input.reshape(1, half_rows, GZ, model_width)
    encoded_grid = encoded.reshape(1, half_rows, GZ, model_width)
    joined = jnp.concatenate(
        [upsample(encoded_grid, deep_weight), upsample(input_grid, skip_weight)], axis=-1
    )
    lower_half = position % 2 == 0
    boundary = jnp.where(lower_half, joined[:, -1:], joined[:, :1])
    partner = swapped(boundary, "seq", 0)
    zero_plane = jnp.zeros_like(partner)
    low_rim = jnp.where(lower_half, zero_plane, partner)
    high_rim = jnp.where(lower_half, partner, zero_plane)
    extended = jnp.concatenate([low_rim, joined, high_rim], axis=1)
    full_xy = jnp.concatenate(
        [plane_send(extended[-1:], 2), extended, plane_send(extended[:1], -2)], axis=0
    )
    decoded = convolve(full_xy, conv_kernel)[None]
    return (encoded, decoded)


def solution(mesh):
    return jax.shard_map(
        body,
        mesh=mesh,
        in_specs=(P(("groups", "seq"), None), P(), P(), P(), P(), P(), P()),
        out_specs=(P(("groups", "seq"), None), P(("groups", "seq"), None, None, None, None)),
        check_vma=False,
    )
```

```python
import math

import jax
import jax.numpy as jnp
from jax import lax
from jax.experimental import pallas as pl
from jax.sharding import PartitionSpec as P

HEADS = 12
GZ = 8


epsilon = 1e-06
leak_slope = 0.01


def shifted(block, axis, distance):
    devices = range(lax.axis_size(axis))
    route = [(i - distance, i) for i in devices if i - distance in devices]
    return lax.ppermute(block, axis, route)


def swapped(x, axis, distance):
    return lax.ppermute(x, axis, [(i, i ^ 1 << distance) for i in range(lax.axis_size(axis))])


def layer_norm(inputs, gain):
    values32 = inputs.astype(jnp.float32)
    row_mean = jnp.mean(values32, axis=-1, keepdims=True)
    centered = values32 - row_mean
    row_var = jnp.mean(centered * centered, axis=-1, keepdims=True)
    return centered * lax.rsqrt(row_var + epsilon) * gain.astype(jnp.float32)


def to_voxels(flat_out, channels):
    extent_x, extent_y, extent_z = (flat_out.shape[0], flat_out.shape[1], flat_out.shape[2])
    shaped = flat_out.reshape(extent_x, extent_y, extent_z, 2, 2, 2, channels)
    shaped = shaped.transpose(0, 3, 1, 4, 2, 5, 6)
    return shaped.reshape(2 * extent_x, 2 * extent_y, 2 * extent_z, channels)


def upsample(token_grid, weight):
    model_width = token_grid.shape[-1]
    product = jnp.dot(
        token_grid.reshape(-1, model_width), weight, preferred_element_type=jnp.float32
    )
    flat_out = product.astype(jnp.bfloat16).reshape(token_grid.shape[:3] + (weight.shape[1],))
    return to_voxels(flat_out, weight.shape[1] // 8)


def convolve(full_xy, conv_kernel):
    accumulated = lax.conv_general_dilated(
        full_xy[None],
        conv_kernel,
        window_strides=(1, 1, 1),
        padding=((0, 0), (0, 0), (1, 1)),
        dimension_numbers=("NDHWC", "DHWIO", "NDHWC"),
        preferred_element_type=jnp.float32,
    )[0]
    activated = jnp.where(accumulated > 0, accumulated, leak_slope * accumulated)
    return activated.astype(jnp.bfloat16)


def plane_send(plane, offset):
    return shifted(plane, "seq", offset)


def attention_kernel(*refs, head_size, score_scale, chunks):
    q_ref = refs[0]
    k_refs = refs[1 : 1 + chunks]
    v_refs = refs[1 + chunks : 1 + 2 * chunks]
    o_ref, lse_ref = refs[-2:]
    pair = q_ref.shape[-1]
    lane = lax.broadcasted_iota(jnp.int32, (1, pair), 1)
    q = q_ref[...]
    result = None
    log_sum = None
    for h in range(pair // head_size):
        in_head = (lane >= h * head_size) & (lane < (h + 1) * head_size)
        q_h = jnp.where(in_head, q, jnp.zeros_like(q))
        scores = [
            lax.dot_general(
                q_h, k_ref[...], (((1,), (1,)), ((), ())), preferred_element_type=jnp.float32
            )
            * score_scale
            for k_ref in k_refs
        ]
        row_max = scores[0].max(axis=-1, keepdims=True)
        for block in scores[1:]:
            row_max = jnp.maximum(row_max, block.max(axis=-1, keepdims=True))
        denominator = None
        numerator = None
        for block, v_ref in zip(scores, v_refs):
            exp_scores = jnp.exp(block - row_max)
            part_sum = jnp.sum(exp_scores, axis=-1, keepdims=True)
            part = jnp.dot(
                exp_scores.astype(jnp.bfloat16), v_ref[...], preferred_element_type=jnp.float32
            )
            denominator = part_sum if denominator is None else denominator + part_sum
            numerator = part if numerator is None else numerator + part
        head_out = numerator / denominator
        head_lse = row_max + jnp.log(denominator)
        result = head_out if result is None else jnp.where(in_head, head_out, result)
        log_sum = (
            jnp.broadcast_to(head_lse, result.shape)
            if log_sum is None
            else jnp.where(in_head, head_lse, log_sum)
        )
    o_ref[...] = result.astype(o_ref.dtype)
    lse_ref[...] = log_sum


def attention(queries, kv_chunks, head_size, score_scale, out_dtype):
    token_count, model_width = queries.shape
    pair = 2 * head_size
    pairs = model_width // pair
    chunks = len(kv_chunks)
    kernel = lambda *refs: attention_kernel(
        *refs, head_size=head_size, score_scale=score_scale, chunks=chunks
    )
    key_specs = [pl.BlockSpec((c.shape[0], pair), lambda j: (0, j)) for c in kv_chunks]
    value_specs = [pl.BlockSpec((c.shape[0], pair), lambda j: (0, j + pairs)) for c in kv_chunks]
    row_spec = pl.BlockSpec((token_count, pair), lambda j: (0, j))
    output, log_sum = pl.pallas_call(
        kernel,
        grid=(pairs,),
        in_specs=[row_spec] + key_specs + value_specs,
        out_specs=[row_spec, row_spec],
        out_shape=[
            jax.ShapeDtypeStruct((token_count, model_width), out_dtype),
            jax.ShapeDtypeStruct((token_count, model_width), jnp.float32),
        ],
    )(queries, *kv_chunks, *kv_chunks)
    return output, log_sum[:, ::head_size]


def exchanged(x, mask):
    devices = lax.axis_size("seq")
    return lax.ppermute(x, "seq", [(i, i ^ mask) for i in range(devices)])


def projected(rows, norm_gain, weight):
    normed = layer_norm(rows, norm_gain).astype(jnp.bfloat16)
    return jnp.dot(normed, weight, preferred_element_type=jnp.float32).astype(jnp.bfloat16)


def body(layer_input, norm_gain, projection, output_weight, deep_weight, skip_weight, conv_kernel):
    token_count, model_width = layer_input.shape
    head_size = model_width // HEADS
    score_scale = 1.0 / math.sqrt(head_size)
    half = lax.axis_size("seq") // 2
    queries = projected(layer_input, norm_gain, projection[:, :model_width])
    mirrored_queries = exchanged(queries, half)
    same_core = [layer_input] + [exchanged(layer_input, mask) for mask in range(2, half, 2)]
    mine = jnp.concatenate(same_core, axis=0)
    theirs = exchanged(mine, 1)
    kv_weight = projection[:, model_width:]
    kv_chunks = [projected(mine, norm_gain, kv_weight), projected(theirs, norm_gain, kv_weight)]
    remote_out, remote_lse = attention(
        mirrored_queries, kv_chunks, head_size, score_scale, jnp.bfloat16
    )
    other_out = exchanged(remote_out, half)
    other_lse = exchanged(remote_lse, half)
    own_out, own_lse = attention(queries, kv_chunks, head_size, score_scale, jnp.float32)
    top = jnp.maximum(own_lse, other_lse)
    own_weight = jnp.repeat(jnp.exp(own_lse - top), head_size, axis=1)
    other_weight = jnp.repeat(jnp.exp(other_lse - top), head_size, axis=1)
    attended = (
        (own_weight * own_out + other_weight * other_out.astype(jnp.float32))
        / (own_weight + other_weight)
    ).astype(jnp.bfloat16)
    encoded = (
        layer_input.astype(jnp.float32)
        + jnp.dot(attended, output_weight, preferred_element_type=jnp.float32)
    ).astype(jnp.bfloat16)
    position = lax.axis_index("seq")
    half_rows = token_count // GZ
    input_grid = layer_input.reshape(1, half_rows, GZ, model_width)
    encoded_grid = encoded.reshape(1, half_rows, GZ, model_width)
    joined = jnp.concatenate(
        [upsample(encoded_grid, deep_weight), upsample(input_grid, skip_weight)], axis=-1
    )
    lower_half = position % 2 == 0
    boundary = jnp.where(lower_half, joined[:, -1:], joined[:, :1])
    partner = swapped(boundary, "seq", 0)
    zero_plane = jnp.zeros_like(partner)
    low_rim = jnp.where(lower_half, zero_plane, partner)
    high_rim = jnp.where(lower_half, partner, zero_plane)
    extended = jnp.concatenate([low_rim, joined, high_rim], axis=1)
    full_xy = jnp.concatenate(
        [plane_send(extended[-1:], 2), extended, plane_send(extended[:1], -2)], axis=0
    )
    decoded = convolve(full_xy, conv_kernel)[None]
    return (encoded, decoded)


def solution(mesh):
    return jax.shard_map(
        body,
        mesh=mesh,
        in_specs=(P(("groups", "seq"), None), P(), P(), P(), P(), P(), P()),
        out_specs=(P(("groups", "seq"), None), P(("groups", "seq"), None, None, None, None)),
        check_vma=False,
    )
```

```python
import math

import jax
import jax.numpy as jnp
from jax import lax
from jax.experimental import pallas as pl
from jax.experimental.pallas import tpu as pltpu
from jax.sharding import PartitionSpec as P

HEADS = 12
GZ = 8


epsilon = 1e-06
leak_slope = 0.01


def shifted(block, axis, distance):
    devices = range(lax.axis_size(axis))
    route = [(i - distance, i) for i in devices if i - distance in devices]
    return lax.ppermute(block, axis, route)


def swapped(x, axis, distance):
    return lax.ppermute(x, axis, [(i, i ^ 1 << distance) for i in range(lax.axis_size(axis))])


def layer_norm(inputs, gain):
    values32 = inputs.astype(jnp.float32)
    row_mean = jnp.mean(values32, axis=-1, keepdims=True)
    centered = values32 - row_mean
    row_var = jnp.mean(centered * centered, axis=-1, keepdims=True)
    return centered * lax.rsqrt(row_var + epsilon) * gain.astype(jnp.float32)


def to_voxels(flat_out, channels):
    extent_x, extent_y, extent_z = (flat_out.shape[0], flat_out.shape[1], flat_out.shape[2])
    shaped = flat_out.reshape(extent_x, extent_y, extent_z, 2, 2, 2, channels)
    shaped = shaped.transpose(0, 3, 1, 4, 2, 5, 6)
    return shaped.reshape(2 * extent_x, 2 * extent_y, 2 * extent_z, channels)


def upsample(token_grid, weight):
    model_width = token_grid.shape[-1]
    product = jnp.dot(
        token_grid.reshape(-1, model_width), weight, preferred_element_type=jnp.float32
    )
    flat_out = product.astype(jnp.bfloat16).reshape(token_grid.shape[:3] + (weight.shape[1],))
    return to_voxels(flat_out, weight.shape[1] // 8)


def convolve(full_xy, conv_kernel):
    accumulated = lax.conv_general_dilated(
        full_xy[None],
        conv_kernel,
        window_strides=(1, 1, 1),
        padding=((0, 0), (0, 0), (1, 1)),
        dimension_numbers=("NDHWC", "DHWIO", "NDHWC"),
        preferred_element_type=jnp.float32,
    )[0]
    activated = jnp.where(accumulated > 0, accumulated, leak_slope * accumulated)
    return activated.astype(jnp.bfloat16)


def plane_send(plane, offset):
    return shifted(plane, "seq", offset)


def attention_kernel(*refs, head_size, score_scale, chunks, whole_output, ordered):
    if ordered:
        refs = refs[:-3] + refs[-2:]
    q_ref = refs[0]
    k_refs = refs[1 : 1 + chunks]
    v_refs = refs[1 + chunks : 1 + 2 * chunks]
    o_ref, lse_ref = refs[-2:]
    step = pl.program_id(0)
    pair = q_ref.shape[-1]
    lane = lax.broadcasted_iota(jnp.int32, (1, pair), 1)
    stat_lane = lax.broadcasted_iota(jnp.int32, (1, lse_ref.shape[-1]), 1)

    @pl.when(step == 0)
    def _():
        lse_ref[...] = jnp.zeros_like(lse_ref)

    q = q_ref[...]
    result = None
    log_sum = lse_ref[...]
    heads = pair // head_size
    for h in range(heads):
        in_head = (lane >= h * head_size) & (lane < (h + 1) * head_size)
        q_h = jnp.where(in_head, q, jnp.zeros_like(q))
        scores = [
            lax.dot_general(
                q_h, k_ref[...], (((1,), (1,)), ((), ())), preferred_element_type=jnp.float32
            )
            * score_scale
            for k_ref in k_refs
        ]
        row_max = scores[0].max(axis=-1, keepdims=True)
        for block in scores[1:]:
            row_max = jnp.maximum(row_max, block.max(axis=-1, keepdims=True))
        denominator = None
        numerator = None
        for block, v_ref in zip(scores, v_refs):
            exp_scores = jnp.exp(block - row_max)
            part_sum = jnp.sum(exp_scores, axis=-1, keepdims=True)
            part = jnp.dot(
                exp_scores.astype(jnp.bfloat16), v_ref[...], preferred_element_type=jnp.float32
            )
            denominator = part_sum if denominator is None else denominator + part_sum
            numerator = part if numerator is None else numerator + part
        head_out = numerator / denominator
        head_lse = row_max + jnp.log(denominator)
        result = head_out if result is None else jnp.where(in_head, head_out, result)
        log_sum = jnp.where(stat_lane == step * heads + h, head_lse, log_sum)
    if whole_output:
        o_ref[:, pl.ds(pl.multiple_of(step * pair, pair), pair)] = result.astype(o_ref.dtype)
    else:
        o_ref[...] = result.astype(o_ref.dtype)
    lse_ref[...] = log_sum


def attention(queries, kv_chunks, head_size, score_scale, out_dtype, whole_output, after=None):
    token_count, model_width = queries.shape
    pair = 2 * head_size
    pairs = model_width // pair
    chunks = len(kv_chunks)
    kernel = lambda *refs: attention_kernel(
        *refs,
        head_size=head_size,
        score_scale=score_scale,
        chunks=chunks,
        whole_output=whole_output,
        ordered=after is not None,
    )
    key_specs = [pl.BlockSpec((c.shape[0], pair), lambda j: (0, j)) for c in kv_chunks]
    value_specs = [pl.BlockSpec((c.shape[0], pair), lambda j: (0, j + pairs)) for c in kv_chunks]
    row_spec = pl.BlockSpec((token_count, pair), lambda j: (0, j))
    stat_width = 128
    if whole_output:
        out_specs = [
            pl.BlockSpec(memory_space=pltpu.VMEM),
            pl.BlockSpec(memory_space=pltpu.VMEM),
        ]
    else:
        out_specs = [row_spec, pl.BlockSpec((token_count, stat_width), lambda j: (0, 0))]
    extra = [] if after is None else [after]
    extra_specs = [pl.BlockSpec(memory_space=pl.ANY) for _ in extra]
    keys = sum(c.shape[0] for c in kv_chunks)
    cost = pl.CostEstimate(
        flops=8 * token_count * keys * model_width,
        transcendentals=token_count * keys * (model_width // head_size),
        bytes_accessed=2 * keys * 2 * model_width + 8 * token_count * model_width,
    )
    output, log_sum = pl.pallas_call(
        kernel,
        grid=(pairs,),
        cost_estimate=cost,
        in_specs=[row_spec] + key_specs + value_specs + extra_specs,
        out_specs=out_specs,
        out_shape=[
            jax.ShapeDtypeStruct((token_count, model_width), out_dtype),
            jax.ShapeDtypeStruct((token_count, stat_width), jnp.float32),
        ],
    )(queries, *kv_chunks, *kv_chunks, *extra)
    return output, log_sum


def exchanged(x, mask):
    devices = lax.axis_size("seq")
    return lax.ppermute(x, "seq", [(i, i ^ mask) for i in range(devices)])


def projected(rows, norm_gain, weight):
    normed = layer_norm(rows, norm_gain).astype(jnp.bfloat16)
    return jnp.dot(normed, weight, preferred_element_type=jnp.float32).astype(jnp.bfloat16)


def body(layer_input, norm_gain, projection, output_weight, deep_weight, skip_weight, conv_kernel):
    token_count, model_width = layer_input.shape
    head_size = model_width // HEADS
    score_scale = 1.0 / math.sqrt(head_size)
    half = lax.axis_size("seq") // 2
    queries = projected(layer_input, norm_gain, projection[:, :model_width])
    mirrored_queries = exchanged(queries, half)
    same_core = [layer_input] + [exchanged(layer_input, mask) for mask in range(2, half, 2)]
    mine = jnp.concatenate(same_core, axis=0)
    theirs = exchanged(mine, 1)
    kv_weight = projection[:, model_width:]
    kv_chunks = [projected(mine, norm_gain, kv_weight), projected(theirs, norm_gain, kv_weight)]
    remote_out, remote_lse = attention(
        mirrored_queries, kv_chunks, head_size, score_scale, jnp.float32, False
    )
    remote_out = remote_out.astype(jnp.bfloat16)
    other_out = exchanged(remote_out, half)
    other_lse = exchanged(remote_lse, half)
    own_out, own_lse = attention(
        queries, kv_chunks, head_size, score_scale, jnp.float32, False, after=remote_out
    )
    heads = model_width // head_size
    top = jnp.maximum(own_lse, other_lse)
    own_weight = jnp.repeat(jnp.exp(own_lse - top)[:, :heads], head_size, axis=1)
    other_weight = jnp.repeat(jnp.exp(other_lse - top)[:, :heads], head_size, axis=1)
    attended = (
        (own_weight * own_out + other_weight * other_out.astype(jnp.float32))
        / (own_weight + other_weight)
    ).astype(jnp.bfloat16)
    encoded = (
        layer_input.astype(jnp.float32)
        + jnp.dot(attended, output_weight, preferred_element_type=jnp.float32)
    ).astype(jnp.bfloat16)
    position = lax.axis_index("seq")
    half_rows = token_count // GZ
    input_grid = layer_input.reshape(1, half_rows, GZ, model_width)
    encoded_grid = encoded.reshape(1, half_rows, GZ, model_width)
    joined = jnp.concatenate(
        [upsample(encoded_grid, deep_weight), upsample(input_grid, skip_weight)], axis=-1
    )
    lower_half = position % 2 == 0
    boundary = jnp.where(lower_half, joined[:, -1:], joined[:, :1])
    partner = swapped(boundary, "seq", 0)
    zero_plane = jnp.zeros_like(partner)
    low_rim = jnp.where(lower_half, zero_plane, partner)
    high_rim = jnp.where(lower_half, partner, zero_plane)
    extended = jnp.concatenate([low_rim, joined, high_rim], axis=1)
    full_xy = jnp.concatenate(
        [plane_send(extended[-1:], 2), extended, plane_send(extended[:1], -2)], axis=0
    )
    decoded = convolve(full_xy, conv_kernel)[None]
    return (encoded, decoded)


def solution(mesh):
    return jax.shard_map(
        body,
        mesh=mesh,
        in_specs=(P(("groups", "seq"), None), P(), P(), P(), P(), P(), P()),
        out_specs=(P(("groups", "seq"), None), P(("groups", "seq"), None, None, None, None)),
        check_vma=False,
    )
```

```python
import math

import jax
import jax.numpy as jnp
from jax import lax
from jax.experimental import pallas as pl
from jax.experimental.pallas import tpu as pltpu
from jax.sharding import PartitionSpec as P

HEADS = 12
GZ = 8


epsilon = 1e-06
leak_slope = 0.01


def shifted(block, axis, distance):
    devices = range(lax.axis_size(axis))
    route = [(i - distance, i) for i in devices if i - distance in devices]
    return lax.ppermute(block, axis, route)


def swapped(x, axis, distance):
    return lax.ppermute(x, axis, [(i, i ^ 1 << distance) for i in range(lax.axis_size(axis))])


def layer_norm(inputs, gain):
    values32 = inputs.astype(jnp.float32)
    row_mean = jnp.mean(values32, axis=-1, keepdims=True)
    centered = values32 - row_mean
    row_var = jnp.mean(centered * centered, axis=-1, keepdims=True)
    return centered * lax.rsqrt(row_var + epsilon) * gain.astype(jnp.float32)


def to_voxels(flat_out, channels):
    extent_x, extent_y, extent_z = (flat_out.shape[0], flat_out.shape[1], flat_out.shape[2])
    shaped = flat_out.reshape(extent_x, extent_y, extent_z, 2, 2, 2, channels)
    shaped = shaped.transpose(0, 3, 1, 4, 2, 5, 6)
    return shaped.reshape(2 * extent_x, 2 * extent_y, 2 * extent_z, channels)


def upsample(token_grid, weight):
    model_width = token_grid.shape[-1]
    product = jnp.dot(
        token_grid.reshape(-1, model_width), weight, preferred_element_type=jnp.float32
    )
    flat_out = product.astype(jnp.bfloat16).reshape(token_grid.shape[:3] + (weight.shape[1],))
    return to_voxels(flat_out, weight.shape[1] // 8)


def convolve(extended, low_plane, high_plane, conv_kernel):
    def conv(field, kernel, x_pad):
        return lax.conv_general_dilated(
            field[None],
            kernel,
            window_strides=(1, 1, 1),
            padding=((x_pad, x_pad), (0, 0), (1, 1)),
            dimension_numbers=("NDHWC", "DHWIO", "NDHWC"),
            preferred_element_type=jnp.float32,
        )[0]

    interior = conv(extended, conv_kernel, 1)
    rims = jnp.concatenate(
        [conv(low_plane, conv_kernel[:1], 0), conv(high_plane, conv_kernel[2:], 0)], axis=0
    )
    accumulated = interior + rims
    activated = jnp.where(accumulated > 0, accumulated, leak_slope * accumulated)
    return activated.astype(jnp.bfloat16)


def plane_send(plane, offset):
    return shifted(plane, "seq", offset)


def attention_kernel(*refs, head_size, score_scale, chunks, whole_output, ordered):
    if ordered:
        refs = refs[:-3] + refs[-2:]
    q_ref = refs[0]
    k_refs = refs[1 : 1 + chunks]
    v_refs = refs[1 + chunks : 1 + 2 * chunks]
    o_ref, lse_ref = refs[-2:]
    step = pl.program_id(0)
    pair = q_ref.shape[-1]
    lane = lax.broadcasted_iota(jnp.int32, (1, pair), 1)
    stat_lane = lax.broadcasted_iota(jnp.int32, (1, lse_ref.shape[-1]), 1)

    @pl.when(step == 0)
    def _():
        lse_ref[...] = jnp.zeros_like(lse_ref)

    q = q_ref[...]
    result = None
    log_sum = lse_ref[...]
    heads = pair // head_size
    for h in range(heads):
        in_head = (lane >= h * head_size) & (lane < (h + 1) * head_size)
        q_h = jnp.where(in_head, q, jnp.zeros_like(q))
        scores = [
            lax.dot_general(
                q_h, k_ref[...], (((1,), (1,)), ((), ())), preferred_element_type=jnp.float32
            )
            * score_scale
            for k_ref in k_refs
        ]
        row_max = scores[0].max(axis=-1, keepdims=True)
        for block in scores[1:]:
            row_max = jnp.maximum(row_max, block.max(axis=-1, keepdims=True))
        denominator = None
        numerator = None
        for block, v_ref in zip(scores, v_refs):
            exp_scores = jnp.exp(block - row_max)
            part_sum = jnp.sum(exp_scores, axis=-1, keepdims=True)
            part = jnp.dot(
                exp_scores.astype(jnp.bfloat16), v_ref[...], preferred_element_type=jnp.float32
            )
            denominator = part_sum if denominator is None else denominator + part_sum
            numerator = part if numerator is None else numerator + part
        head_out = numerator / denominator
        head_lse = row_max + jnp.log(denominator)
        result = head_out if result is None else jnp.where(in_head, head_out, result)
        log_sum = jnp.where(stat_lane == step * heads + h, head_lse, log_sum)
    if whole_output:
        o_ref[:, pl.ds(pl.multiple_of(step * pair, pair), pair)] = result.astype(o_ref.dtype)
    else:
        o_ref[...] = result.astype(o_ref.dtype)
    lse_ref[...] = log_sum


def attention(queries, kv_chunks, head_size, score_scale, out_dtype, whole_output, after=None):
    token_count, model_width = queries.shape
    pair = 2 * head_size
    pairs = model_width // pair
    chunks = len(kv_chunks)
    kernel = lambda *refs: attention_kernel(
        *refs,
        head_size=head_size,
        score_scale=score_scale,
        chunks=chunks,
        whole_output=whole_output,
        ordered=after is not None,
    )
    key_specs = [pl.BlockSpec((c.shape[0], pair), lambda j: (0, j)) for c in kv_chunks]
    value_specs = [pl.BlockSpec((c.shape[0], pair), lambda j: (0, j + pairs)) for c in kv_chunks]
    row_spec = pl.BlockSpec((token_count, pair), lambda j: (0, j))
    stat_width = 128
    if whole_output:
        out_specs = [
            pl.BlockSpec(memory_space=pltpu.VMEM),
            pl.BlockSpec(memory_space=pltpu.VMEM),
        ]
    else:
        out_specs = [row_spec, pl.BlockSpec((token_count, stat_width), lambda j: (0, 0))]
    extra = [] if after is None else [after]
    extra_specs = [pl.BlockSpec(memory_space=pl.ANY) for _ in extra]
    keys = sum(c.shape[0] for c in kv_chunks)
    cost = pl.CostEstimate(
        flops=8 * token_count * keys * model_width,
        transcendentals=token_count * keys * (model_width // head_size),
        bytes_accessed=2 * keys * 2 * model_width + 8 * token_count * model_width,
    )
    output, log_sum = pl.pallas_call(
        kernel,
        grid=(pairs,),
        cost_estimate=cost,
        in_specs=[row_spec] + key_specs + value_specs + extra_specs,
        out_specs=out_specs,
        out_shape=[
            jax.ShapeDtypeStruct((token_count, model_width), out_dtype),
            jax.ShapeDtypeStruct((token_count, stat_width), jnp.float32),
        ],
    )(queries, *kv_chunks, *kv_chunks, *extra)
    return output, log_sum


def exchanged(x, mask):
    devices = lax.axis_size("seq")
    return lax.ppermute(x, "seq", [(i, i ^ mask) for i in range(devices)])


def projected(rows, norm_gain, weight):
    normed = layer_norm(rows, norm_gain).astype(jnp.bfloat16)
    return jnp.dot(normed, weight, preferred_element_type=jnp.float32).astype(jnp.bfloat16)


def body(layer_input, norm_gain, projection, output_weight, deep_weight, skip_weight, conv_kernel):
    token_count, model_width = layer_input.shape
    head_size = model_width // HEADS
    score_scale = 1.0 / math.sqrt(head_size)
    half = lax.axis_size("seq") // 2
    queries = projected(layer_input, norm_gain, projection[:, :model_width])
    mirrored_queries = exchanged(queries, half)
    same_core = [layer_input] + [exchanged(layer_input, mask) for mask in range(2, half, 2)]
    mine = jnp.concatenate(same_core, axis=0)
    theirs = exchanged(mine, 1)
    kv_weight = projection[:, model_width:]
    kv_chunks = [projected(mine, norm_gain, kv_weight), projected(theirs, norm_gain, kv_weight)]
    remote_out, remote_lse = attention(
        mirrored_queries, kv_chunks, head_size, score_scale, jnp.bfloat16, False
    )
    other_out = exchanged(remote_out, half)
    other_lse = exchanged(remote_lse, half)
    own_out, own_lse = attention(
        queries, kv_chunks, head_size, score_scale, jnp.float32, False, after=remote_out
    )
    heads = model_width // head_size
    top = jnp.maximum(own_lse, other_lse)
    own_weight = jnp.repeat(jnp.exp(own_lse - top)[:, :heads], head_size, axis=1)
    other_weight = jnp.repeat(jnp.exp(other_lse - top)[:, :heads], head_size, axis=1)
    attended = (
        (own_weight * own_out + other_weight * other_out.astype(jnp.float32))
        / (own_weight + other_weight)
    ).astype(jnp.bfloat16)
    encoded = (
        layer_input.astype(jnp.float32)
        + jnp.dot(attended, output_weight, preferred_element_type=jnp.float32)
    ).astype(jnp.bfloat16)
    position = lax.axis_index("seq")
    half_rows = token_count // GZ
    input_grid = layer_input.reshape(1, half_rows, GZ, model_width)
    encoded_grid = encoded.reshape(1, half_rows, GZ, model_width)
    joined = jnp.concatenate(
        [upsample(encoded_grid, deep_weight), upsample(input_grid, skip_weight)], axis=-1
    )
    lower_half = position % 2 == 0
    boundary = jnp.where(lower_half, joined[:, -1:], joined[:, :1])
    partner = swapped(boundary, "seq", 0)
    zero_plane = jnp.zeros_like(partner)
    low_rim = jnp.where(lower_half, zero_plane, partner)
    high_rim = jnp.where(lower_half, partner, zero_plane)
    extended = jnp.concatenate([low_rim, joined, high_rim], axis=1)
    low_plane = plane_send(extended[-1:], 2)
    high_plane = plane_send(extended[:1], -2)
    decoded = convolve(extended, low_plane, high_plane, conv_kernel)[None]
    return (encoded, decoded)


def solution(mesh):
    return jax.shard_map(
        body,
        mesh=mesh,
        in_specs=(P(("groups", "seq"), None), P(), P(), P(), P(), P(), P()),
        out_specs=(P(("groups", "seq"), None), P(("groups", "seq"), None, None, None, None)),
        check_vma=False,
    )
```

```python
import math

import jax
import jax.numpy as jnp
from jax import lax
from jax.experimental import pallas as pl
from jax.experimental.pallas import tpu as pltpu
from jax.sharding import PartitionSpec as P

HEADS = 12
GZ = 8


epsilon = 1e-06
leak_slope = 0.01


def shifted(block, axis, distance):
    devices = range(lax.axis_size(axis))
    route = [(i - distance, i) for i in devices if i - distance in devices]
    return lax.ppermute(block, axis, route)


def swapped(x, axis, distance):
    return lax.ppermute(x, axis, [(i, i ^ 1 << distance) for i in range(lax.axis_size(axis))])


def layer_norm(inputs, gain):
    values32 = inputs.astype(jnp.float32)
    row_mean = jnp.mean(values32, axis=-1, keepdims=True)
    centered = values32 - row_mean
    row_var = jnp.mean(centered * centered, axis=-1, keepdims=True)
    return centered * lax.rsqrt(row_var + epsilon) * gain.astype(jnp.float32)


def to_voxels(flat_out, channels):
    extent_x, extent_y, extent_z = (flat_out.shape[0], flat_out.shape[1], flat_out.shape[2])
    shaped = flat_out.reshape(extent_x, extent_y, extent_z, 2, 2, 2, channels)
    shaped = shaped.transpose(0, 3, 1, 4, 2, 5, 6)
    return shaped.reshape(2 * extent_x, 2 * extent_y, 2 * extent_z, channels)


def upsample(token_grid, weight):
    model_width = token_grid.shape[-1]
    product = jnp.dot(
        token_grid.reshape(-1, model_width), weight, preferred_element_type=jnp.float32
    )
    flat_out = product.astype(jnp.bfloat16).reshape(token_grid.shape[:3] + (weight.shape[1],))
    return to_voxels(flat_out, weight.shape[1] // 8)


def convolve(extended, low_plane, high_plane, conv_kernel):
    def conv(field, kernel, x_pad):
        return lax.conv_general_dilated(
            field[None],
            kernel,
            window_strides=(1, 1, 1),
            padding=((x_pad, x_pad), (0, 0), (1, 1)),
            dimension_numbers=("NDHWC", "DHWIO", "NDHWC"),
            preferred_element_type=jnp.float32,
        )[0]

    interior = lax.optimization_barrier(conv(extended, conv_kernel, 1))
    rims = jnp.concatenate(
        [conv(low_plane, conv_kernel[:1], 0), conv(high_plane, conv_kernel[2:], 0)], axis=0
    )
    accumulated = interior + rims
    activated = jnp.where(accumulated > 0, accumulated, leak_slope * accumulated)
    return activated.astype(jnp.bfloat16)


def plane_send(plane, offset):
    return shifted(plane, "seq", offset)


def attention_kernel(*refs, head_size, score_scale, chunks, whole_output, ordered):
    if ordered:
        refs = refs[:-3] + refs[-2:]
    q_ref = refs[0]
    k_refs = refs[1 : 1 + chunks]
    v_refs = refs[1 + chunks : 1 + 2 * chunks]
    o_ref, lse_ref = refs[-2:]
    step = pl.program_id(0)
    pair = q_ref.shape[-1]
    lane = lax.broadcasted_iota(jnp.int32, (1, pair), 1)
    stat_lane = lax.broadcasted_iota(jnp.int32, (1, lse_ref.shape[-1]), 1)

    @pl.when(step == 0)
    def _():
        lse_ref[...] = jnp.zeros_like(lse_ref)

    q = q_ref[...]
    result = None
    log_sum = lse_ref[...]
    heads = pair // head_size
    for h in range(heads):
        in_head = (lane >= h * head_size) & (lane < (h + 1) * head_size)
        q_h = jnp.where(in_head, q, jnp.zeros_like(q))
        scores = [
            lax.dot_general(
                q_h, k_ref[...], (((1,), (1,)), ((), ())), preferred_element_type=jnp.float32
            )
            for k_ref in k_refs
        ]
        raw_max = scores[0].max(axis=-1, keepdims=True)
        for block in scores[1:]:
            raw_max = jnp.maximum(raw_max, block.max(axis=-1, keepdims=True))
        row_max = raw_max * score_scale
        denominator = None
        numerator = None
        for block, v_ref in zip(scores, v_refs):
            exp_scores = jnp.exp2((block - raw_max) * (score_scale * math.log2(math.e)))
            part_sum = jnp.sum(exp_scores, axis=-1, keepdims=True)
            part = jnp.dot(
                exp_scores.astype(jnp.bfloat16), v_ref[...], preferred_element_type=jnp.float32
            )
            denominator = part_sum if denominator is None else denominator + part_sum
            numerator = part if numerator is None else numerator + part
        head_out = numerator / denominator
        head_lse = row_max + jnp.log(denominator)
        result = head_out if result is None else jnp.where(in_head, head_out, result)
        log_sum = jnp.where(stat_lane == step * heads + h, head_lse, log_sum)
    if whole_output:
        o_ref[:, pl.ds(pl.multiple_of(step * pair, pair), pair)] = result.astype(o_ref.dtype)
    else:
        o_ref[...] = result.astype(o_ref.dtype)
    lse_ref[...] = log_sum


def attention(queries, kv_chunks, head_size, score_scale, out_dtype, whole_output, after=None):
    token_count, model_width = queries.shape
    pair = 2 * head_size
    pairs = model_width // pair
    chunks = len(kv_chunks)
    kernel = lambda *refs: attention_kernel(
        *refs,
        head_size=head_size,
        score_scale=score_scale,
        chunks=chunks,
        whole_output=whole_output,
        ordered=after is not None,
    )
    key_specs = [pl.BlockSpec((c.shape[0], pair), lambda j: (0, j)) for c in kv_chunks]
    value_specs = [pl.BlockSpec((c.shape[0], pair), lambda j: (0, j + pairs)) for c in kv_chunks]
    row_spec = pl.BlockSpec((token_count, pair), lambda j: (0, j))
    stat_width = 128
    if whole_output:
        out_specs = [
            pl.BlockSpec(memory_space=pltpu.VMEM),
            pl.BlockSpec(memory_space=pltpu.VMEM),
        ]
    else:
        out_specs = [row_spec, pl.BlockSpec((token_count, stat_width), lambda j: (0, 0))]
    extra = [] if after is None else [after]
    extra_specs = [pl.BlockSpec(memory_space=pl.ANY) for _ in extra]
    keys = sum(c.shape[0] for c in kv_chunks)
    cost = pl.CostEstimate(
        flops=8 * token_count * keys * model_width,
        transcendentals=token_count * keys * (model_width // head_size),
        bytes_accessed=2 * keys * 2 * model_width + 8 * token_count * model_width,
    )
    output, log_sum = pl.pallas_call(
        kernel,
        grid=(pairs,),
        cost_estimate=cost,
        in_specs=[row_spec] + key_specs + value_specs + extra_specs,
        out_specs=out_specs,
        out_shape=[
            jax.ShapeDtypeStruct((token_count, model_width), out_dtype),
            jax.ShapeDtypeStruct((token_count, stat_width), jnp.float32),
        ],
    )(queries, *kv_chunks, *kv_chunks, *extra)
    return output, log_sum


def exchanged(x, mask):
    devices = lax.axis_size("seq")
    return lax.ppermute(x, "seq", [(i, i ^ mask) for i in range(devices)])


def projected(rows, norm_gain, weight):
    normed = layer_norm(rows, norm_gain).astype(jnp.bfloat16)
    return jnp.dot(normed, weight, preferred_element_type=jnp.float32).astype(jnp.bfloat16)


def body(layer_input, norm_gain, projection, output_weight, deep_weight, skip_weight, conv_kernel):
    token_count, model_width = layer_input.shape
    head_size = model_width // HEADS
    score_scale = 1.0 / math.sqrt(head_size)
    half = lax.axis_size("seq") // 2
    queries = projected(layer_input, norm_gain, projection[:, :model_width])
    mirrored_queries = exchanged(queries, half)
    same_core = [layer_input] + [exchanged(layer_input, mask) for mask in range(2, half, 2)]
    mine = jnp.concatenate(same_core, axis=0)
    theirs = exchanged(mine, 1)
    kv_weight = projection[:, model_width:]
    kv_chunks = [projected(mine, norm_gain, kv_weight), projected(theirs, norm_gain, kv_weight)]
    remote_out, remote_lse = attention(
        mirrored_queries, kv_chunks, head_size, score_scale, jnp.bfloat16, False
    )
    other_out = exchanged(remote_out, half)
    other_lse = exchanged(remote_lse, half)
    own_out, own_lse = attention(
        queries, kv_chunks, head_size, score_scale, jnp.float32, False, after=remote_out
    )
    heads = model_width // head_size
    top = jnp.maximum(own_lse, other_lse)
    own_weight = jnp.repeat(jnp.exp(own_lse - top)[:, :heads], head_size, axis=1)
    other_weight = jnp.repeat(jnp.exp(other_lse - top)[:, :heads], head_size, axis=1)
    attended = (
        (own_weight * own_out + other_weight * other_out.astype(jnp.float32))
        / (own_weight + other_weight)
    ).astype(jnp.bfloat16)
    encoded = (
        layer_input.astype(jnp.float32)
        + jnp.dot(attended, output_weight, preferred_element_type=jnp.float32)
    ).astype(jnp.bfloat16)
    position = lax.axis_index("seq")
    half_rows = token_count // GZ
    input_grid = layer_input.reshape(1, half_rows, GZ, model_width)
    encoded_grid = encoded.reshape(1, half_rows, GZ, model_width)
    joined = jnp.concatenate(
        [upsample(encoded_grid, deep_weight), upsample(input_grid, skip_weight)], axis=-1
    )
    lower_half = position % 2 == 0
    boundary = jnp.where(lower_half, joined[:, -1:], joined[:, :1])
    partner = swapped(boundary, "seq", 0)
    zero_plane = jnp.zeros_like(partner)
    low_rim = jnp.where(lower_half, zero_plane, partner)
    high_rim = jnp.where(lower_half, partner, zero_plane)
    extended = jnp.concatenate([low_rim, joined, high_rim], axis=1)
    low_plane = plane_send(extended[-1:], 2)
    high_plane = plane_send(extended[:1], -2)
    decoded = convolve(extended, low_plane, high_plane, conv_kernel)[None]
    return (encoded, decoded)


def solution(mesh):
    return jax.shard_map(
        body,
        mesh=mesh,
        in_specs=(P(("groups", "seq"), None), P(), P(), P(), P(), P(), P()),
        out_specs=(P(("groups", "seq"), None), P(("groups", "seq"), None, None, None, None)),
        check_vma=False,
    )
```

```python
import math

import jax
import jax.numpy as jnp
from jax import lax
from jax.experimental import pallas as pl
from jax.experimental.pallas import tpu as pltpu
from jax.experimental.layout import Layout, with_layout_constraint
from jax.sharding import PartitionSpec as P

HEADS = 12
GZ = 8


epsilon = 1e-06
leak_slope = 0.01


def shifted(block, axis, distance):
    devices = range(lax.axis_size(axis))
    route = [(i - distance, i) for i in devices if i - distance in devices]
    return lax.ppermute(block, axis, route)


def swapped(x, axis, distance):
    return lax.ppermute(x, axis, [(i, i ^ 1 << distance) for i in range(lax.axis_size(axis))])


def layer_norm(inputs, gain):
    values32 = inputs.astype(jnp.float32)
    row_mean = jnp.mean(values32, axis=-1, keepdims=True)
    centered = values32 - row_mean
    row_var = jnp.mean(centered * centered, axis=-1, keepdims=True)
    return centered * lax.rsqrt(row_var + epsilon) * gain.astype(jnp.float32)


def to_voxels(flat_out, channels):
    extent_x, extent_y, extent_z = (flat_out.shape[0], flat_out.shape[1], flat_out.shape[2])
    shaped = flat_out.reshape(extent_x, extent_y, extent_z, 2, 2, 2, channels)
    shaped = shaped.transpose(0, 3, 1, 4, 2, 5, 6)
    return shaped.reshape(2 * extent_x, 2 * extent_y, 2 * extent_z, channels)


def upsample(token_grid, weight):
    model_width = token_grid.shape[-1]
    product = jnp.dot(
        token_grid.reshape(-1, model_width), weight, preferred_element_type=jnp.float32
    )
    flat_out = product.astype(jnp.bfloat16).reshape(token_grid.shape[:3] + (weight.shape[1],))
    return to_voxels(flat_out, weight.shape[1] // 8)


def convolve(extended, low_plane, high_plane, conv_kernel):
    def conv(field, kernel, x_pad):
        return lax.conv_general_dilated(
            field[None],
            kernel,
            window_strides=(1, 1, 1),
            padding=((x_pad, x_pad), (0, 0), (1, 1)),
            dimension_numbers=("NDHWC", "DHWIO", "NDHWC"),
            preferred_element_type=jnp.float32,
        )[0]

    interior = lax.optimization_barrier(conv(extended, conv_kernel, 1))
    rims = jnp.concatenate(
        [conv(low_plane, conv_kernel[:1], 0), conv(high_plane, conv_kernel[2:], 0)], axis=0
    )
    accumulated = interior + rims
    activated = jnp.where(accumulated > 0, accumulated, leak_slope * accumulated)
    return activated.astype(jnp.bfloat16)


def plane_send(plane, offset):
    return shifted(plane, "seq", offset)


def attention_kernel(*refs, head_size, score_scale, chunks, whole_output, ordered, rows_out):
    rows_ref = None
    if rows_out:
        rows_ref = refs[-1]
        refs = refs[:-1]
    if ordered:
        refs = refs[:-3] + refs[-2:]
    q_ref = refs[0]
    k_refs = refs[1 : 1 + chunks]
    v_refs = refs[1 + chunks : 1 + 2 * chunks]
    o_ref, lse_ref = refs[-2:]
    step = pl.program_id(0)
    pair = q_ref.shape[-1]
    lane = lax.broadcasted_iota(jnp.int32, (1, pair), 1)
    stat_lane = lax.broadcasted_iota(jnp.int32, (1, lse_ref.shape[-1]), 1)

    @pl.when(step == 0)
    def _():
        lse_ref[...] = jnp.zeros_like(lse_ref)

    q = q_ref[...]
    result = None
    log_sum = lse_ref[...]
    heads = pair // head_size
    for h in range(heads):
        in_head = (lane >= h * head_size) & (lane < (h + 1) * head_size)
        q_h = jnp.where(in_head, q, jnp.zeros_like(q))
        scores = [
            lax.dot_general(
                q_h, k_ref[...], (((1,), (1,)), ((), ())), preferred_element_type=jnp.float32
            )
            for k_ref in k_refs
        ]
        raw_max = scores[0].max(axis=-1, keepdims=True)
        for block in scores[1:]:
            raw_max = jnp.maximum(raw_max, block.max(axis=-1, keepdims=True))
        row_max = raw_max * score_scale
        denominator = None
        numerator = None
        for block, v_ref in zip(scores, v_refs):
            exp_scores = jnp.exp2((block - raw_max) * (score_scale * math.log2(math.e)))
            part_sum = jnp.sum(exp_scores, axis=-1, keepdims=True)
            part = jnp.dot(
                exp_scores.astype(jnp.bfloat16), v_ref[...], preferred_element_type=jnp.float32
            )
            denominator = part_sum if denominator is None else denominator + part_sum
            numerator = part if numerator is None else numerator + part
        head_out = numerator / denominator
        head_lse = row_max + jnp.log(denominator)
        result = head_out if result is None else jnp.where(in_head, head_out, result)
        log_sum = jnp.where(stat_lane == step * heads + h, head_lse, log_sum)
    if whole_output:
        o_ref[:, pl.ds(pl.multiple_of(step * pair, pair), pair)] = result.astype(o_ref.dtype)
    else:
        o_ref[...] = result.astype(o_ref.dtype)
    lse_ref[...] = log_sum
    if rows_out:

        @pl.when(step == pl.num_programs(0) - 1)
        def _():
            rows_ref[...] = jnp.transpose(log_sum)[: rows_ref.shape[0]]


def attention(
    queries, kv_chunks, head_size, score_scale, out_dtype, whole_output, after=None, rows_out=False
):
    token_count, model_width = queries.shape
    pair = 2 * head_size
    pairs = model_width // pair
    chunks = len(kv_chunks)
    kernel = lambda *refs: attention_kernel(
        *refs,
        head_size=head_size,
        score_scale=score_scale,
        chunks=chunks,
        whole_output=whole_output,
        ordered=after is not None,
        rows_out=rows_out,
    )
    key_specs = [pl.BlockSpec((c.shape[0], pair), lambda j: (0, j)) for c in kv_chunks]
    value_specs = [pl.BlockSpec((c.shape[0], pair), lambda j: (0, j + pairs)) for c in kv_chunks]
    row_spec = pl.BlockSpec((token_count, pair), lambda j: (0, j))
    stat_width = 128
    if whole_output:
        out_specs = [
            pl.BlockSpec(memory_space=pltpu.VMEM),
            pl.BlockSpec(memory_space=pltpu.VMEM),
        ]
    else:
        out_specs = [row_spec, pl.BlockSpec((token_count, stat_width), lambda j: (0, 0))]
    extra = [] if after is None else [after]
    extra_specs = [pl.BlockSpec(memory_space=pl.ANY) for _ in extra]
    keys = sum(c.shape[0] for c in kv_chunks)
    cost = pl.CostEstimate(
        flops=8 * token_count * keys * model_width,
        transcendentals=token_count * keys * (model_width // head_size),
        bytes_accessed=2 * keys * 2 * model_width + 8 * token_count * model_width,
    )
    heads = model_width // head_size
    stat_rows = -(-heads // 8) * 8
    if rows_out:
        out_specs = out_specs + [pl.BlockSpec((stat_rows, stat_width), lambda j: (0, 0))]
    out_shape = [
        jax.ShapeDtypeStruct((token_count, model_width), out_dtype),
        jax.ShapeDtypeStruct((token_count, stat_width), jnp.float32),
    ]
    if rows_out:
        out_shape.append(jax.ShapeDtypeStruct((stat_rows, stat_width), jnp.float32))
    results = pl.pallas_call(
        kernel,
        grid=(pairs,),
        cost_estimate=cost,
        in_specs=[row_spec] + key_specs + value_specs + extra_specs,
        out_specs=out_specs,
        out_shape=out_shape,
    )(queries, *kv_chunks, *kv_chunks, *extra)
    if rows_out:
        return results[0], results[2]
    return results[0], results[1]


def exchanged(x, mask):
    devices = lax.axis_size("seq")
    return lax.ppermute(x, "seq", [(i, i ^ mask) for i in range(devices)])


def projected(rows, norm_gain, weight):
    normed = layer_norm(rows, norm_gain).astype(jnp.bfloat16)
    return jnp.dot(normed, weight, preferred_element_type=jnp.float32).astype(jnp.bfloat16)


def body(layer_input, norm_gain, projection, output_weight, deep_weight, skip_weight, conv_kernel):
    token_count, model_width = layer_input.shape
    head_size = model_width // HEADS
    score_scale = 1.0 / math.sqrt(head_size)
    half = lax.axis_size("seq") // 2
    queries = projected(layer_input, norm_gain, projection[:, :model_width])
    mirrored_queries = exchanged(queries, half)
    same_core = [layer_input] + [exchanged(layer_input, mask) for mask in range(2, half, 2)]
    mine = jnp.concatenate(same_core, axis=0)
    theirs = exchanged(mine, 1)
    kv_weight = projection[:, model_width:]
    kv_chunks = [projected(mine, norm_gain, kv_weight), projected(theirs, norm_gain, kv_weight)]
    remote_out, remote_lse = attention(
        mirrored_queries, kv_chunks, head_size, score_scale, jnp.bfloat16, False, rows_out=True
    )
    heads = model_width // head_size
    other_out = exchanged(remote_out, half)
    row_major = Layout(major_to_minor=(0, 1))
    sent_lse = with_layout_constraint(remote_lse, row_major)
    other_lse = with_layout_constraint(exchanged(sent_lse, half), row_major)[:heads].T
    own_out, own_lse = attention(
        queries, kv_chunks, head_size, score_scale, jnp.float32, False, after=remote_out
    )
    own_lse = own_lse[:, :heads]
    top = jnp.maximum(own_lse, other_lse) + 0 * other_out[:1, :1].astype(jnp.float32)
    own_weight = jnp.repeat(jnp.exp(own_lse - top), head_size, axis=1)
    other_weight = jnp.repeat(jnp.exp(other_lse - top), head_size, axis=1)
    attended = (
        (own_weight * own_out + other_weight * other_out.astype(jnp.float32))
        / (own_weight + other_weight)
    ).astype(jnp.bfloat16)
    encoded = (
        layer_input.astype(jnp.float32)
        + jnp.dot(attended, output_weight, preferred_element_type=jnp.float32)
    ).astype(jnp.bfloat16)
    position = lax.axis_index("seq")
    half_rows = token_count // GZ
    input_grid = layer_input.reshape(1, half_rows, GZ, model_width)
    encoded_grid = encoded.reshape(1, half_rows, GZ, model_width)
    joined = jnp.concatenate(
        [upsample(encoded_grid, deep_weight), upsample(input_grid, skip_weight)], axis=-1
    )
    lower_half = position % 2 == 0
    boundary = jnp.where(lower_half, joined[:, -1:], joined[:, :1])
    partner = swapped(boundary, "seq", 0)
    zero_plane = jnp.zeros_like(partner)
    low_rim = jnp.where(lower_half, zero_plane, partner)
    high_rim = jnp.where(lower_half, partner, zero_plane)
    extended = jnp.concatenate([low_rim, joined, high_rim], axis=1)
    low_plane = plane_send(extended[-1:], 2)
    high_plane = plane_send(extended[:1], -2)
    decoded = convolve(extended, low_plane, high_plane, conv_kernel)[None]
    return (encoded, decoded)


def solution(mesh):
    return jax.shard_map(
        body,
        mesh=mesh,
        in_specs=(P(("groups", "seq"), None), P(), P(), P(), P(), P(), P()),
        out_specs=(P(("groups", "seq"), None), P(("groups", "seq"), None, None, None, None)),
        check_vma=False,
    )
```

```python
import math

import jax
import jax.numpy as jnp
from jax import lax
from jax.experimental import pallas as pl
from jax.experimental.pallas import tpu as pltpu
from jax.experimental.layout import Layout, with_layout_constraint
from jax.sharding import PartitionSpec as P

HEADS = 12
GZ = 8


epsilon = 1e-06
leak_slope = 0.01


def shifted(block, axis, distance):
    devices = range(lax.axis_size(axis))
    route = [(i - distance, i) for i in devices if i - distance in devices]
    return lax.ppermute(block, axis, route)


def swapped(x, axis, distance):
    return lax.ppermute(x, axis, [(i, i ^ 1 << distance) for i in range(lax.axis_size(axis))])


def layer_norm(inputs, gain):
    values32 = inputs.astype(jnp.float32)
    row_mean = jnp.mean(values32, axis=-1, keepdims=True)
    centered = values32 - row_mean
    row_var = jnp.mean(centered * centered, axis=-1, keepdims=True)
    return centered * lax.rsqrt(row_var + epsilon) * gain.astype(jnp.float32)


def to_voxels(flat_out, channels):
    extent_x, extent_y, extent_z = (flat_out.shape[0], flat_out.shape[1], flat_out.shape[2])
    shaped = flat_out.reshape(extent_x, extent_y, extent_z, 2, 2, 2, channels)
    shaped = shaped.transpose(0, 3, 1, 4, 2, 5, 6)
    return shaped.reshape(2 * extent_x, 2 * extent_y, 2 * extent_z, channels)


def upsample(token_grid, weight):
    model_width = token_grid.shape[-1]
    product = jnp.dot(
        token_grid.reshape(-1, model_width), weight, preferred_element_type=jnp.float32
    )
    flat_out = product.astype(jnp.bfloat16).reshape(token_grid.shape[:3] + (weight.shape[1],))
    return to_voxels(flat_out, weight.shape[1] // 8)


def convolve(extended, low_plane, high_plane, conv_kernel):
    def conv(field, kernel, x_pad):
        return lax.conv_general_dilated(
            field[None],
            kernel,
            window_strides=(1, 1, 1),
            padding=((x_pad, x_pad), (0, 0), (1, 1)),
            dimension_numbers=("NDHWC", "DHWIO", "NDHWC"),
            preferred_element_type=jnp.float32,
        )[0]

    interior = lax.optimization_barrier(conv(extended, conv_kernel, 1))
    rims = jnp.concatenate(
        [conv(low_plane, conv_kernel[:1], 0), conv(high_plane, conv_kernel[2:], 0)], axis=0
    )
    accumulated = interior + rims
    activated = jnp.where(accumulated > 0, accumulated, leak_slope * accumulated)
    return activated.astype(jnp.bfloat16)


def plane_send(plane, offset):
    return shifted(plane, "seq", offset)


def attention_kernel(*refs, head_size, score_scale, chunks, whole_output, ordered, rows_out):
    rows_ref = None
    if rows_out:
        rows_ref = refs[-1]
        refs = refs[:-1]
    if ordered:
        refs = refs[: -2 - ordered] + refs[-2:]
    q_ref = refs[0]
    k_refs = refs[1 : 1 + chunks]
    v_refs = refs[1 + chunks : 1 + 2 * chunks]
    o_ref, lse_ref = refs[-2:]
    step = pl.program_id(0)
    pair = q_ref.shape[-1]
    lane = lax.broadcasted_iota(jnp.int32, (1, pair), 1)
    stat_lane = lax.broadcasted_iota(jnp.int32, (1, lse_ref.shape[-1]), 1)

    @pl.when(step == 0)
    def _():
        lse_ref[...] = jnp.zeros_like(lse_ref)

    q = q_ref[...]
    result = None
    log_sum = lse_ref[...]
    heads = pair // head_size
    for h in range(heads):
        in_head = (lane >= h * head_size) & (lane < (h + 1) * head_size)
        q_h = jnp.where(in_head, q, jnp.zeros_like(q))
        scores = [
            lax.dot_general(
                q_h, k_ref[...], (((1,), (1,)), ((), ())), preferred_element_type=jnp.float32
            )
            for k_ref in k_refs
        ]
        raw_max = scores[0].max(axis=-1, keepdims=True)
        for block in scores[1:]:
            raw_max = jnp.maximum(raw_max, block.max(axis=-1, keepdims=True))
        row_max = raw_max * score_scale
        denominator = None
        numerator = None
        for block, v_ref in zip(scores, v_refs):
            exp_scores = jnp.exp2((block - raw_max) * (score_scale * math.log2(math.e)))
            part_sum = jnp.sum(exp_scores, axis=-1, keepdims=True)
            part = jnp.dot(
                exp_scores.astype(jnp.bfloat16), v_ref[...], preferred_element_type=jnp.float32
            )
            denominator = part_sum if denominator is None else denominator + part_sum
            numerator = part if numerator is None else numerator + part
        head_out = numerator / denominator
        head_lse = row_max + jnp.log(denominator)
        result = head_out if result is None else jnp.where(in_head, head_out, result)
        log_sum = jnp.where(stat_lane == step * heads + h, head_lse, log_sum)
    if whole_output:
        o_ref[:, pl.ds(pl.multiple_of(step * pair, pair), pair)] = result.astype(o_ref.dtype)
    else:
        o_ref[...] = result.astype(o_ref.dtype)
    lse_ref[...] = log_sum
    if rows_out:

        @pl.when(step == pl.num_programs(0) - 1)
        def _():
            rows_ref[...] = jnp.transpose(log_sum)[: rows_ref.shape[0]]


def attention(
    queries, kv_chunks, head_size, score_scale, out_dtype, whole_output, after=None, rows_out=False
):
    token_count, model_width = queries.shape
    pair = 2 * head_size
    pairs = model_width // pair
    chunks = len(kv_chunks)
    kernel = lambda *refs: attention_kernel(
        *refs,
        head_size=head_size,
        score_scale=score_scale,
        chunks=chunks,
        whole_output=whole_output,
        ordered=0 if after is None else len(after),
        rows_out=rows_out,
    )
    key_specs = [pl.BlockSpec((c.shape[0], pair), lambda j: (0, j)) for c in kv_chunks]
    value_specs = [pl.BlockSpec((c.shape[0], pair), lambda j: (0, j + pairs)) for c in kv_chunks]
    row_spec = pl.BlockSpec((token_count, pair), lambda j: (0, j))
    stat_width = 128
    if whole_output:
        out_specs = [
            pl.BlockSpec(memory_space=pltpu.VMEM),
            pl.BlockSpec(memory_space=pltpu.VMEM),
        ]
    else:
        out_specs = [row_spec, pl.BlockSpec((token_count, stat_width), lambda j: (0, 0))]
    extra = [] if after is None else list(after)
    extra_specs = [pl.BlockSpec(memory_space=pl.ANY) for _ in extra]
    keys = sum(c.shape[0] for c in kv_chunks)
    cost = pl.CostEstimate(
        flops=8 * token_count * keys * model_width,
        transcendentals=token_count * keys * (model_width // head_size),
        bytes_accessed=2 * keys * 2 * model_width + 8 * token_count * model_width,
    )
    heads = model_width // head_size
    stat_rows = -(-heads // 8) * 8
    if rows_out:
        out_specs = out_specs + [pl.BlockSpec((stat_rows, stat_width), lambda j: (0, 0))]
    out_shape = [
        jax.ShapeDtypeStruct((token_count, model_width), out_dtype),
        jax.ShapeDtypeStruct((token_count, stat_width), jnp.float32),
    ]
    if rows_out:
        out_shape.append(jax.ShapeDtypeStruct((stat_rows, stat_width), jnp.float32))
    results = pl.pallas_call(
        kernel,
        grid=(pairs,),
        cost_estimate=cost,
        in_specs=[row_spec] + key_specs + value_specs + extra_specs,
        out_specs=out_specs,
        out_shape=out_shape,
    )(queries, *kv_chunks, *kv_chunks, *extra)
    if rows_out:
        return results[0], results[2]
    return results[0], results[1]


def exchanged(x, mask):
    devices = lax.axis_size("seq")
    return lax.ppermute(x, "seq", [(i, i ^ mask) for i in range(devices)])


def projected(rows, norm_gain, weight):
    normed = layer_norm(rows, norm_gain).astype(jnp.bfloat16)
    return jnp.dot(normed, weight, preferred_element_type=jnp.float32).astype(jnp.bfloat16)


def body(layer_input, norm_gain, projection, output_weight, deep_weight, skip_weight, conv_kernel):
    token_count, model_width = layer_input.shape
    head_size = model_width // HEADS
    score_scale = 1.0 / math.sqrt(head_size)
    half = lax.axis_size("seq") // 2
    position = lax.axis_index("seq")
    half_rows = token_count // GZ
    input_grid = layer_input.reshape(1, half_rows, GZ, model_width)
    lower_half = position % 2 == 0

    def with_rims(voxels):
        boundary = jnp.where(lower_half, voxels[:, -1:], voxels[:, :1])
        partner = swapped(boundary, "seq", 0)
        zero_plane = jnp.zeros_like(partner)
        low_rim = jnp.where(lower_half, zero_plane, partner)
        high_rim = jnp.where(lower_half, partner, zero_plane)
        extended = jnp.concatenate([low_rim, voxels, high_rim], axis=1)
        return extended, plane_send(extended[-1:], 2), plane_send(extended[:1], -2)

    queries = projected(layer_input, norm_gain, projection[:, :model_width])
    mirrored_queries = exchanged(queries, half)
    same_core = [layer_input] + [exchanged(layer_input, mask) for mask in range(2, half, 2)]
    mine = jnp.concatenate(same_core, axis=0)
    theirs = exchanged(mine, 1)
    kv_weight = projection[:, model_width:]
    kv_chunks = [projected(mine, norm_gain, kv_weight), projected(theirs, norm_gain, kv_weight)]
    remote_out, remote_lse = attention(
        mirrored_queries, kv_chunks, head_size, score_scale, jnp.bfloat16, False, rows_out=True
    )
    heads = model_width // head_size
    other_out = exchanged(remote_out, half)
    row_major = Layout(major_to_minor=(0, 1))
    sent_lse = with_layout_constraint(remote_lse, row_major)
    other_lse = with_layout_constraint(exchanged(sent_lse, half), row_major)[:heads].T
    skip_parts = with_rims(upsample(layer_input.reshape(1, half_rows, GZ, model_width), skip_weight))
    own_out, own_lse = attention(
        queries,
        kv_chunks,
        head_size,
        score_scale,
        jnp.float32,
        False,
        after=[remote_out, skip_parts[1], skip_parts[2]],
    )
    own_lse = own_lse[:, :heads]
    top = jnp.maximum(own_lse, other_lse) + 0 * other_out[:1, :1].astype(jnp.float32)
    own_weight = jnp.repeat(jnp.exp(own_lse - top), head_size, axis=1)
    other_weight = jnp.repeat(jnp.exp(other_lse - top), head_size, axis=1)
    attended = (
        (own_weight * own_out + other_weight * other_out.astype(jnp.float32))
        / (own_weight + other_weight)
    ).astype(jnp.bfloat16)
    encoded = (
        layer_input.astype(jnp.float32)
        + jnp.dot(attended, output_weight, preferred_element_type=jnp.float32)
    ).astype(jnp.bfloat16)
    encoded_grid = encoded.reshape(1, half_rows, GZ, model_width)
    deep_parts = with_rims(upsample(encoded_grid, deep_weight))
    extended, low_plane, high_plane = [
        jnp.concatenate([deep, skip], axis=-1) for deep, skip in zip(deep_parts, skip_parts)
    ]
    decoded = convolve(extended, low_plane, high_plane, conv_kernel)[None]
    return (encoded, decoded)


def solution(mesh):
    return jax.shard_map(
        body,
        mesh=mesh,
        in_specs=(P(("groups", "seq"), None), P(), P(), P(), P(), P(), P()),
        out_specs=(P(("groups", "seq"), None), P(("groups", "seq"), None, None, None, None)),
        check_vma=False,
    )
```

```python
import math

import jax
import jax.numpy as jnp
from jax import lax
from jax.experimental import pallas as pl
from jax.experimental.pallas import tpu as pltpu
from jax.experimental.layout import Layout, with_layout_constraint
from jax.sharding import PartitionSpec as P

HEADS = 12
GZ = 8


epsilon = 1e-06
leak_slope = 0.01


def shifted(block, axis, distance):
    devices = range(lax.axis_size(axis))
    route = [(i - distance, i) for i in devices if i - distance in devices]
    return lax.ppermute(block, axis, route)


def swapped(x, axis, distance):
    return lax.ppermute(x, axis, [(i, i ^ 1 << distance) for i in range(lax.axis_size(axis))])


def layer_norm(inputs, gain):
    values32 = inputs.astype(jnp.float32)
    row_mean = jnp.mean(values32, axis=-1, keepdims=True)
    centered = values32 - row_mean
    row_var = jnp.mean(centered * centered, axis=-1, keepdims=True)
    return centered * lax.rsqrt(row_var + epsilon) * gain.astype(jnp.float32)


def to_voxels(flat_out, channels):
    extent_x, extent_y, extent_z = (flat_out.shape[0], flat_out.shape[1], flat_out.shape[2])
    shaped = flat_out.reshape(extent_x, extent_y, extent_z, 2, 2, 2, channels)
    shaped = shaped.transpose(0, 3, 1, 4, 2, 5, 6)
    return shaped.reshape(2 * extent_x, 2 * extent_y, 2 * extent_z, channels)


def upsample(token_grid, weight):
    model_width = token_grid.shape[-1]
    product = jnp.dot(
        token_grid.reshape(-1, model_width), weight, preferred_element_type=jnp.float32
    )
    flat_out = product.astype(jnp.bfloat16).reshape(token_grid.shape[:3] + (weight.shape[1],))
    return to_voxels(flat_out, weight.shape[1] // 8)


def convolve(extended, low_plane, high_plane, conv_kernel):
    def conv(field, kernel, x_pad):
        return lax.conv_general_dilated(
            field[None],
            kernel,
            window_strides=(1, 1, 1),
            padding=((x_pad, x_pad), (0, 0), (1, 1)),
            dimension_numbers=("NDHWC", "DHWIO", "NDHWC"),
            preferred_element_type=jnp.float32,
        )[0]

    interior = lax.optimization_barrier(conv(extended, conv_kernel, 1))
    rims = jnp.concatenate(
        [conv(low_plane, conv_kernel[:1], 0), conv(high_plane, conv_kernel[2:], 0)], axis=0
    )
    accumulated = interior + rims
    activated = jnp.where(accumulated > 0, accumulated, leak_slope * accumulated)
    return activated.astype(jnp.bfloat16)


def plane_send(plane, offset):
    return shifted(plane, "seq", offset)


def corner_send(row, offset):
    devices = range(lax.axis_size("seq"))
    route = [(i, (i ^ 1) + offset) for i in devices if (i ^ 1) + offset in devices]
    return lax.ppermute(row, "seq", route)


def attention_kernel(*refs, head_size, score_scale, chunks, whole_output, ordered, rows_out):
    rows_ref = None
    if rows_out:
        rows_ref = refs[-1]
        refs = refs[:-1]
    if ordered:
        refs = refs[:-3] + refs[-2:]
    q_ref = refs[0]
    k_refs = refs[1 : 1 + chunks]
    v_refs = refs[1 + chunks : 1 + 2 * chunks]
    o_ref, lse_ref = refs[-2:]
    step = pl.program_id(0)
    pair = q_ref.shape[-1]
    lane = lax.broadcasted_iota(jnp.int32, (1, pair), 1)
    stat_lane = lax.broadcasted_iota(jnp.int32, (1, lse_ref.shape[-1]), 1)

    @pl.when(step == 0)
    def _():
        lse_ref[...] = jnp.zeros_like(lse_ref)

    q = q_ref[...]
    result = None
    log_sum = lse_ref[...]
    heads = pair // head_size
    for h in range(heads):
        in_head = (lane >= h * head_size) & (lane < (h + 1) * head_size)
        q_h = jnp.where(in_head, q, jnp.zeros_like(q))
        scores = [
            lax.dot_general(
                q_h, k_ref[...], (((1,), (1,)), ((), ())), preferred_element_type=jnp.float32
            )
            for k_ref in k_refs
        ]
        raw_max = scores[0].max(axis=-1, keepdims=True)
        for block in scores[1:]:
            raw_max = jnp.maximum(raw_max, block.max(axis=-1, keepdims=True))
        row_max = raw_max * score_scale
        denominator = None
        numerator = None
        for block, v_ref in zip(scores, v_refs):
            exp_scores = jnp.exp2((block - raw_max) * (score_scale * math.log2(math.e)))
            part_sum = jnp.sum(exp_scores, axis=-1, keepdims=True)
            part = jnp.dot(
                exp_scores.astype(jnp.bfloat16), v_ref[...], preferred_element_type=jnp.float32
            )
            denominator = part_sum if denominator is None else denominator + part_sum
            numerator = part if numerator is None else numerator + part
        head_out = numerator / denominator
        head_lse = row_max + jnp.log(denominator)
        result = head_out if result is None else jnp.where(in_head, head_out, result)
        log_sum = jnp.where(stat_lane == step * heads + h, head_lse, log_sum)
    if whole_output:
        o_ref[:, pl.ds(pl.multiple_of(step * pair, pair), pair)] = result.astype(o_ref.dtype)
    else:
        o_ref[...] = result.astype(o_ref.dtype)
    lse_ref[...] = log_sum
    if rows_out:

        @pl.when(step == pl.num_programs(0) - 1)
        def _():
            rows_ref[...] = jnp.transpose(log_sum)[: rows_ref.shape[0]]


def attention(
    queries, kv_chunks, head_size, score_scale, out_dtype, whole_output, after=None, rows_out=False
):
    token_count, model_width = queries.shape
    pair = 2 * head_size
    pairs = model_width // pair
    chunks = len(kv_chunks)
    kernel = lambda *refs: attention_kernel(
        *refs,
        head_size=head_size,
        score_scale=score_scale,
        chunks=chunks,
        whole_output=whole_output,
        ordered=after is not None,
        rows_out=rows_out,
    )
    key_specs = [pl.BlockSpec((c.shape[0], pair), lambda j: (0, j)) for c in kv_chunks]
    value_specs = [pl.BlockSpec((c.shape[0], pair), lambda j: (0, j + pairs)) for c in kv_chunks]
    row_spec = pl.BlockSpec((token_count, pair), lambda j: (0, j))
    stat_width = 128
    if whole_output:
        out_specs = [
            pl.BlockSpec(memory_space=pltpu.VMEM),
            pl.BlockSpec(memory_space=pltpu.VMEM),
        ]
    else:
        out_specs = [row_spec, pl.BlockSpec((token_count, stat_width), lambda j: (0, 0))]
    extra = [] if after is None else [after]
    extra_specs = [pl.BlockSpec(memory_space=pl.ANY) for _ in extra]
    keys = sum(c.shape[0] for c in kv_chunks)
    cost = pl.CostEstimate(
        flops=8 * token_count * keys * model_width,
        transcendentals=token_count * keys * (model_width // head_size),
        bytes_accessed=2 * keys * 2 * model_width + 8 * token_count * model_width,
    )
    heads = model_width // head_size
    stat_rows = -(-heads // 8) * 8
    if rows_out:
        out_specs = out_specs + [pl.BlockSpec((stat_rows, stat_width), lambda j: (0, 0))]
    out_shape = [
        jax.ShapeDtypeStruct((token_count, model_width), out_dtype),
        jax.ShapeDtypeStruct((token_count, stat_width), jnp.float32),
    ]
    if rows_out:
        out_shape.append(jax.ShapeDtypeStruct((stat_rows, stat_width), jnp.float32))
    results = pl.pallas_call(
        kernel,
        grid=(pairs,),
        cost_estimate=cost,
        in_specs=[row_spec] + key_specs + value_specs + extra_specs,
        out_specs=out_specs,
        out_shape=out_shape,
    )(queries, *kv_chunks, *kv_chunks, *extra)
    if rows_out:
        return results[0], results[2]
    return results[0], results[1]


def exchanged(x, mask):
    devices = lax.axis_size("seq")
    return lax.ppermute(x, "seq", [(i, i ^ mask) for i in range(devices)])


def projected(rows, norm_gain, weight):
    normed = layer_norm(rows, norm_gain).astype(jnp.bfloat16)
    return jnp.dot(normed, weight, preferred_element_type=jnp.float32).astype(jnp.bfloat16)


def body(layer_input, norm_gain, projection, output_weight, deep_weight, skip_weight, conv_kernel):
    token_count, model_width = layer_input.shape
    head_size = model_width // HEADS
    score_scale = 1.0 / math.sqrt(head_size)
    half = lax.axis_size("seq") // 2
    queries = projected(layer_input, norm_gain, projection[:, :model_width])
    mirrored_queries = exchanged(queries, half)
    same_core = [layer_input] + [exchanged(layer_input, mask) for mask in range(2, half, 2)]
    mine = jnp.concatenate(same_core, axis=0)
    theirs = exchanged(mine, 1)
    kv_weight = projection[:, model_width:]
    kv_chunks = [projected(mine, norm_gain, kv_weight), projected(theirs, norm_gain, kv_weight)]
    remote_out, remote_lse = attention(
        mirrored_queries, kv_chunks, head_size, score_scale, jnp.bfloat16, False, rows_out=True
    )
    heads = model_width // head_size
    other_out = exchanged(remote_out, half)
    row_major = Layout(major_to_minor=(0, 1))
    sent_lse = with_layout_constraint(remote_lse, row_major)
    other_lse = with_layout_constraint(exchanged(sent_lse, half), row_major)[:heads].T
    own_out, own_lse = attention(
        queries, kv_chunks, head_size, score_scale, jnp.float32, False, after=remote_out
    )
    own_lse = own_lse[:, :heads]
    top = jnp.maximum(own_lse, other_lse) + 0 * other_out[:1, :1].astype(jnp.float32)
    own_weight = jnp.repeat(jnp.exp(own_lse - top), head_size, axis=1)
    other_weight = jnp.repeat(jnp.exp(other_lse - top), head_size, axis=1)
    attended = (
        (own_weight * own_out + other_weight * other_out.astype(jnp.float32))
        / (own_weight + other_weight)
    ).astype(jnp.bfloat16)
    encoded = (
        layer_input.astype(jnp.float32)
        + jnp.dot(attended, output_weight, preferred_element_type=jnp.float32)
    ).astype(jnp.bfloat16)
    position = lax.axis_index("seq")
    half_rows = token_count // GZ
    input_grid = layer_input.reshape(1, half_rows, GZ, model_width)
    encoded_grid = encoded.reshape(1, half_rows, GZ, model_width)
    joined = jnp.concatenate(
        [upsample(encoded_grid, deep_weight), upsample(input_grid, skip_weight)], axis=-1
    )
    lower_half = position % 2 == 0
    boundary = jnp.where(lower_half, joined[:, -1:], joined[:, :1])
    partner = swapped(boundary, "seq", 0)
    low_plane = plane_send(joined[-1:], 2)
    high_plane = plane_send(joined[:1], -2)
    low_corner = corner_send(boundary[-1:], 2)
    high_corner = corner_send(boundary[:1], -2)

    def rimmed(core, rim):
        zero_plane = jnp.zeros_like(rim)
        low_rim = jnp.where(lower_half, zero_plane, rim)
        high_rim = jnp.where(lower_half, rim, zero_plane)
        return jnp.concatenate([low_rim, core, high_rim], axis=1)

    extended = rimmed(joined, partner)
    decoded = convolve(
        extended, rimmed(low_plane, low_corner), rimmed(high_plane, high_corner), conv_kernel
    )[None]
    return (encoded, decoded)


def solution(mesh):
    return jax.shard_map(
        body,
        mesh=mesh,
        in_specs=(P(("groups", "seq"), None), P(), P(), P(), P(), P(), P()),
        out_specs=(P(("groups", "seq"), None), P(("groups", "seq"), None, None, None, None)),
        check_vma=False,
    )
```

```python
import math

import jax
import jax.numpy as jnp
from jax import lax
from jax.experimental import pallas as pl
from jax.experimental.pallas import tpu as pltpu
from jax.sharding import PartitionSpec as P

HEADS = 12
GZ = 8


epsilon = 1e-06
leak_slope = 0.01


def shifted(block, axis, distance):
    devices = range(lax.axis_size(axis))
    route = [(i - distance, i) for i in devices if i - distance in devices]
    return lax.ppermute(block, axis, route)


def swapped(x, axis, distance):
    return lax.ppermute(x, axis, [(i, i ^ 1 << distance) for i in range(lax.axis_size(axis))])


def layer_norm(inputs, gain):
    values32 = inputs.astype(jnp.float32)
    row_mean = jnp.mean(values32, axis=-1, keepdims=True)
    centered = values32 - row_mean
    row_var = jnp.mean(centered * centered, axis=-1, keepdims=True)
    return centered * lax.rsqrt(row_var + epsilon) * gain.astype(jnp.float32)


def to_voxels(flat_out, channels):
    extent_x, extent_y, extent_z = (flat_out.shape[0], flat_out.shape[1], flat_out.shape[2])
    shaped = flat_out.reshape(extent_x, extent_y, extent_z, 2, 2, 2, channels)
    shaped = shaped.transpose(0, 3, 1, 4, 2, 5, 6)
    return shaped.reshape(2 * extent_x, 2 * extent_y, 2 * extent_z, channels)


def upsample(token_grid, weight):
    model_width = token_grid.shape[-1]
    product = jnp.dot(
        token_grid.reshape(-1, model_width), weight, preferred_element_type=jnp.float32
    )
    flat_out = product.astype(jnp.bfloat16).reshape(token_grid.shape[:3] + (weight.shape[1],))
    return to_voxels(flat_out, weight.shape[1] // 8)


def convolve(extended, low_plane, high_plane, conv_kernel):
    def conv(field, kernel, x_pad):
        return lax.conv_general_dilated(
            field[None],
            kernel,
            window_strides=(1, 1, 1),
            padding=((x_pad, x_pad), (0, 0), (1, 1)),
            dimension_numbers=("NDHWC", "DHWIO", "NDHWC"),
            preferred_element_type=jnp.float32,
        )[0]

    interior = lax.optimization_barrier(conv(extended, conv_kernel, 1))
    rims = jnp.concatenate(
        [conv(low_plane, conv_kernel[:1], 0), conv(high_plane, conv_kernel[2:], 0)], axis=0
    )
    accumulated = interior + rims
    activated = jnp.where(accumulated > 0, accumulated, leak_slope * accumulated)
    return activated.astype(jnp.bfloat16)


def plane_send(plane, offset):
    return shifted(plane, "seq", offset)


def attention_kernel(*refs, head_size, score_scale, chunks, whole_output, ordered, rows_out):
    rows_ref = None
    if rows_out:
        rows_ref = refs[-1]
        refs = refs[:-1]
    if ordered:
        refs = refs[:-3] + refs[-2:]
    q_ref = refs[0]
    k_refs = refs[1 : 1 + chunks]
    v_refs = refs[1 + chunks : 1 + 2 * chunks]
    o_ref, lse_ref = refs[-2:]
    step = pl.program_id(0)
    pair = q_ref.shape[-1]
    lane = lax.broadcasted_iota(jnp.int32, (1, pair), 1)
    stat_lane = lax.broadcasted_iota(jnp.int32, (1, lse_ref.shape[-1]), 1)

    @pl.when(step == 0)
    def _():
        lse_ref[...] = jnp.zeros_like(lse_ref)

    q = q_ref[...]
    result = None
    log_sum = lse_ref[...]
    heads = pair // head_size
    for h in range(heads):
        in_head = (lane >= h * head_size) & (lane < (h + 1) * head_size)
        q_h = jnp.where(in_head, q, jnp.zeros_like(q))
        scores = [
            lax.dot_general(
                q_h, k_ref[...], (((1,), (1,)), ((), ())), preferred_element_type=jnp.float32
            )
            for k_ref in k_refs
        ]
        raw_max = scores[0].max(axis=-1, keepdims=True)
        for block in scores[1:]:
            raw_max = jnp.maximum(raw_max, block.max(axis=-1, keepdims=True))
        row_max = raw_max * score_scale
        denominator = None
        numerator = None
        for block, v_ref in zip(scores, v_refs):
            exp_scores = jnp.exp2((block - raw_max) * (score_scale * math.log2(math.e)))
            part_sum = jnp.sum(exp_scores, axis=-1, keepdims=True)
            part = jnp.dot(
                exp_scores.astype(jnp.bfloat16), v_ref[...], preferred_element_type=jnp.float32
            )
            denominator = part_sum if denominator is None else denominator + part_sum
            numerator = part if numerator is None else numerator + part
        head_out = numerator / denominator
        head_lse = row_max + jnp.log(denominator)
        result = head_out if result is None else jnp.where(in_head, head_out, result)
        log_sum = jnp.where(stat_lane == step * heads + h, head_lse, log_sum)
    if whole_output:
        o_ref[:, pl.ds(pl.multiple_of(step * pair, pair), pair)] = result.astype(o_ref.dtype)
    else:
        o_ref[...] = result.astype(o_ref.dtype)
    lse_ref[...] = log_sum
    if rows_out:

        @pl.when(step == pl.num_programs(0) - 1)
        def _():
            rows_ref[...] = jnp.transpose(log_sum)[: rows_ref.shape[0]]


def attention(
    queries, kv_chunks, head_size, score_scale, out_dtype, whole_output, after=None, rows_out=False
):
    token_count, model_width = queries.shape
    pair = 2 * head_size
    pairs = model_width // pair
    chunks = len(kv_chunks)
    kernel = lambda *refs: attention_kernel(
        *refs,
        head_size=head_size,
        score_scale=score_scale,
        chunks=chunks,
        whole_output=whole_output,
        ordered=after is not None,
        rows_out=rows_out,
    )
    key_specs = [pl.BlockSpec((c.shape[0], pair), lambda j: (0, j)) for c in kv_chunks]
    value_specs = [pl.BlockSpec((c.shape[0], pair), lambda j: (0, j + pairs)) for c in kv_chunks]
    row_spec = pl.BlockSpec((token_count, pair), lambda j: (0, j))
    stat_width = 128
    if whole_output:
        out_specs = [
            pl.BlockSpec(memory_space=pltpu.VMEM),
            pl.BlockSpec(memory_space=pltpu.VMEM),
        ]
    else:
        out_specs = [row_spec, pl.BlockSpec((token_count, stat_width), lambda j: (0, 0))]
    extra = [] if after is None else [after]
    extra_specs = [pl.BlockSpec(memory_space=pl.ANY) for _ in extra]
    keys = sum(c.shape[0] for c in kv_chunks)
    cost = pl.CostEstimate(
        flops=8 * token_count * keys * model_width,
        transcendentals=token_count * keys * (model_width // head_size),
        bytes_accessed=2 * keys * 2 * model_width + 8 * token_count * model_width,
    )
    heads = model_width // head_size
    stat_rows = -(-heads // 8) * 8
    if rows_out:
        out_specs = out_specs + [pl.BlockSpec((stat_rows, stat_width), lambda j: (0, 0))]
    out_shape = [
        jax.ShapeDtypeStruct((token_count, model_width), out_dtype),
        jax.ShapeDtypeStruct((token_count, stat_width), jnp.float32),
    ]
    if rows_out:
        out_shape.append(jax.ShapeDtypeStruct((stat_rows, stat_width), jnp.float32))
    results = pl.pallas_call(
        kernel,
        grid=(pairs,),
        cost_estimate=cost,
        in_specs=[row_spec] + key_specs + value_specs + extra_specs,
        out_specs=out_specs,
        out_shape=out_shape,
    )(queries, *kv_chunks, *kv_chunks, *extra)
    if rows_out:
        return results[0], results[2]
    return results[0], results[1]


def exchanged(x, mask):
    devices = lax.axis_size("seq")
    return lax.ppermute(x, "seq", [(i, i ^ mask) for i in range(devices)])


def projected(rows, norm_gain, weight):
    normed = layer_norm(rows, norm_gain).astype(jnp.bfloat16)
    return jnp.dot(normed, weight, preferred_element_type=jnp.float32).astype(jnp.bfloat16)


def body(layer_input, norm_gain, projection, output_weight, deep_weight, skip_weight, conv_kernel):
    token_count, model_width = layer_input.shape
    head_size = model_width // HEADS
    score_scale = 1.0 / math.sqrt(head_size)
    half = lax.axis_size("seq") // 2
    queries = projected(layer_input, norm_gain, projection[:, :model_width])
    mirrored_queries = exchanged(queries, half)
    same_core = [layer_input] + [exchanged(layer_input, mask) for mask in range(2, half, 2)]
    mine = jnp.concatenate(same_core, axis=0)
    theirs = exchanged(mine, 1)
    kv_weight = projection[:, model_width:]
    kv_chunks = [projected(mine, norm_gain, kv_weight), projected(theirs, norm_gain, kv_weight)]
    remote_out, remote_lse = attention(
        mirrored_queries, kv_chunks, head_size, score_scale, jnp.bfloat16, False, rows_out=True
    )
    heads = model_width // head_size
    parts = []
    remainder = remote_lse
    for _ in range(3):
        part = remainder.astype(jnp.bfloat16)
        parts.append(part)
        remainder = remainder - part.astype(jnp.float32)
    packed = jnp.concatenate(parts, axis=0).reshape(-1, model_width)
    received = exchanged(jnp.concatenate([remote_out, packed], axis=0), half)
    other_out = received[:token_count]
    other_parts = received[token_count:].reshape(3, -1, remote_lse.shape[-1]).astype(jnp.float32)
    other_lse = ((other_parts[0] + other_parts[1]) + other_parts[2])[:heads].T
    own_out, own_lse = attention(
        queries, kv_chunks, head_size, score_scale, jnp.float32, False, after=remote_out
    )
    own_lse = own_lse[:, :heads]
    top = jnp.maximum(own_lse, other_lse) + 0 * other_out[:1, :1].astype(jnp.float32)
    own_weight = jnp.repeat(jnp.exp(own_lse - top), head_size, axis=1)
    other_weight = jnp.repeat(jnp.exp(other_lse - top), head_size, axis=1)
    attended = (
        (own_weight * own_out + other_weight * other_out.astype(jnp.float32))
        / (own_weight + other_weight)
    ).astype(jnp.bfloat16)
    encoded = (
        layer_input.astype(jnp.float32)
        + jnp.dot(attended, output_weight, preferred_element_type=jnp.float32)
    ).astype(jnp.bfloat16)
    position = lax.axis_index("seq")
    half_rows = token_count // GZ
    input_grid = layer_input.reshape(1, half_rows, GZ, model_width)
    encoded_grid = encoded.reshape(1, half_rows, GZ, model_width)
    joined = jnp.concatenate(
        [upsample(encoded_grid, deep_weight), upsample(input_grid, skip_weight)], axis=-1
    )
    lower_half = position % 2 == 0
    boundary = jnp.where(lower_half, joined[:, -1:], joined[:, :1])
    partner = swapped(boundary, "seq", 0)
    zero_plane = jnp.zeros_like(partner)
    low_rim = jnp.where(lower_half, zero_plane, partner)
    high_rim = jnp.where(lower_half, partner, zero_plane)
    extended = jnp.concatenate([low_rim, joined, high_rim], axis=1)
    low_plane = plane_send(extended[-1:], 2)
    high_plane = plane_send(extended[:1], -2)
    decoded = convolve(extended, low_plane, high_plane, conv_kernel)[None]
    return (encoded, decoded)


def solution(mesh):
    return jax.shard_map(
        body,
        mesh=mesh,
        in_specs=(P(("groups", "seq"), None), P(), P(), P(), P(), P(), P()),
        out_specs=(P(("groups", "seq"), None), P(("groups", "seq"), None, None, None, None)),
        check_vma=False,
    )
```

```python
import math

import jax
import jax.numpy as jnp
from jax import lax
from jax.experimental import pallas as pl
from jax.experimental.pallas import tpu as pltpu
from jax.experimental.layout import Layout, with_layout_constraint
from jax.sharding import PartitionSpec as P

HEADS = 12
GZ = 8


epsilon = 1e-06
leak_slope = 0.01


def shifted(block, axis, distance):
    devices = range(lax.axis_size(axis))
    route = [(i - distance, i) for i in devices if i - distance in devices]
    return lax.ppermute(block, axis, route)


def swapped(x, axis, distance):
    return lax.ppermute(x, axis, [(i, i ^ 1 << distance) for i in range(lax.axis_size(axis))])


def layer_norm(inputs, gain):
    values32 = inputs.astype(jnp.float32)
    row_mean = jnp.mean(values32, axis=-1, keepdims=True)
    centered = values32 - row_mean
    row_var = jnp.mean(centered * centered, axis=-1, keepdims=True)
    return centered * lax.rsqrt(row_var + epsilon) * gain.astype(jnp.float32)


def to_voxels(flat_out, channels):
    extent_x, extent_y, extent_z = (flat_out.shape[0], flat_out.shape[1], flat_out.shape[2])
    shaped = flat_out.reshape(extent_x, extent_y, extent_z, 2, 2, 2, channels)
    shaped = shaped.transpose(0, 3, 1, 4, 2, 5, 6)
    return shaped.reshape(2 * extent_x, 2 * extent_y, 2 * extent_z, channels)


def upsample(token_grid, weight):
    model_width = token_grid.shape[-1]
    product = jnp.dot(
        token_grid.reshape(-1, model_width), weight, preferred_element_type=jnp.float32
    )
    flat_out = product.astype(jnp.bfloat16).reshape(token_grid.shape[:3] + (weight.shape[1],))
    return to_voxels(flat_out, weight.shape[1] // 8)


def convolve(extended, low_plane, high_plane, conv_kernel):
    def conv(field, kernel, x_pad):
        return lax.conv_general_dilated(
            field[None],
            kernel,
            window_strides=(1, 1, 1),
            padding=((x_pad, x_pad), (0, 0), (1, 1)),
            dimension_numbers=("NDHWC", "DHWIO", "NDHWC"),
            preferred_element_type=jnp.float32,
        )[0]

    interior = lax.optimization_barrier(conv(extended, conv_kernel, 1))
    rims = jnp.concatenate(
        [conv(low_plane, conv_kernel[:1], 0), conv(high_plane, conv_kernel[2:], 0)], axis=0
    )
    accumulated = interior + rims
    activated = jnp.where(accumulated > 0, accumulated, leak_slope * accumulated)
    return activated.astype(jnp.bfloat16)


def plane_send(plane, offset):
    return shifted(plane, "seq", offset)


def attention_kernel(*refs, head_size, score_scale, chunks, whole_output, ordered, rows_out):
    rows_ref = None
    if rows_out:
        rows_ref = refs[-1]
        refs = refs[:-1]
    if ordered:
        refs = refs[:-3] + refs[-2:]
    q_ref = refs[0]
    k_refs = refs[1 : 1 + chunks]
    v_refs = refs[1 + chunks : 1 + 2 * chunks]
    o_ref, lse_ref = refs[-2:]
    step = pl.program_id(0)
    pair = q_ref.shape[-1]
    lane = lax.broadcasted_iota(jnp.int32, (1, pair), 1)
    stat_lane = lax.broadcasted_iota(jnp.int32, (1, lse_ref.shape[-1]), 1)

    @pl.when(step == 0)
    def _():
        lse_ref[...] = jnp.zeros_like(lse_ref)

    q = q_ref[...]
    result = None
    log_sum = lse_ref[...]
    heads = pair // head_size
    for h in range(heads):
        in_head = (lane >= h * head_size) & (lane < (h + 1) * head_size)
        q_h = jnp.where(in_head, q, jnp.zeros_like(q))
        scores = [
            lax.dot_general(
                q_h, k_ref[...], (((1,), (1,)), ((), ())), preferred_element_type=jnp.float32
            )
            for k_ref in k_refs
        ]
        raw_max = scores[0].max(axis=-1, keepdims=True)
        for block in scores[1:]:
            raw_max = jnp.maximum(raw_max, block.max(axis=-1, keepdims=True))
        row_max = raw_max * score_scale
        denominator = None
        numerator = None
        for block, v_ref in zip(scores, v_refs):
            exp_scores = jnp.exp2((block - raw_max) * (score_scale * math.log2(math.e)))
            part_sum = jnp.sum(exp_scores, axis=-1, keepdims=True)
            part = jnp.dot(
                exp_scores.astype(jnp.bfloat16), v_ref[...], preferred_element_type=jnp.float32
            )
            denominator = part_sum if denominator is None else denominator + part_sum
            numerator = part if numerator is None else numerator + part
        head_out = numerator / denominator
        head_lse = row_max + jnp.log(denominator)
        result = head_out if result is None else jnp.where(in_head, head_out, result)
        log_sum = jnp.where(stat_lane == step * heads + h, head_lse, log_sum)
    if whole_output:
        o_ref[:, pl.ds(pl.multiple_of(step * pair, pair), pair)] = result.astype(o_ref.dtype)
    else:
        o_ref[...] = result.astype(o_ref.dtype)
    lse_ref[...] = log_sum
    if rows_out:

        @pl.when(step == pl.num_programs(0) - 1)
        def _():
            rows_ref[...] = jnp.transpose(log_sum)[: rows_ref.shape[0]]


def attention(
    queries, kv_chunks, head_size, score_scale, out_dtype, whole_output, after=None, rows_out=False
):
    token_count, model_width = queries.shape
    pair = 2 * head_size
    pairs = model_width // pair
    chunks = len(kv_chunks)
    kernel = lambda *refs: attention_kernel(
        *refs,
        head_size=head_size,
        score_scale=score_scale,
        chunks=chunks,
        whole_output=whole_output,
        ordered=after is not None,
        rows_out=rows_out,
    )
    key_specs = [pl.BlockSpec((c.shape[0], pair), lambda j: (0, j)) for c in kv_chunks]
    value_specs = [pl.BlockSpec((c.shape[0], pair), lambda j: (0, j + pairs)) for c in kv_chunks]
    row_spec = pl.BlockSpec((token_count, pair), lambda j: (0, j))
    stat_width = 128
    if whole_output:
        out_specs = [
            pl.BlockSpec(memory_space=pltpu.VMEM),
            pl.BlockSpec(memory_space=pltpu.VMEM),
        ]
    else:
        out_specs = [row_spec, pl.BlockSpec((token_count, stat_width), lambda j: (0, 0))]
    extra = [] if after is None else [after]
    extra_specs = [pl.BlockSpec(memory_space=pl.ANY) for _ in extra]
    keys = sum(c.shape[0] for c in kv_chunks)
    cost = pl.CostEstimate(
        flops=8 * token_count * keys * model_width,
        transcendentals=token_count * keys * (model_width // head_size),
        bytes_accessed=2 * keys * 2 * model_width + 8 * token_count * model_width,
    )
    heads = model_width // head_size
    stat_rows = -(-heads // 8) * 8
    if rows_out:
        out_specs = out_specs + [pl.BlockSpec((stat_rows, stat_width), lambda j: (0, 0))]
    out_shape = [
        jax.ShapeDtypeStruct((token_count, model_width), out_dtype),
        jax.ShapeDtypeStruct((token_count, stat_width), jnp.float32),
    ]
    if rows_out:
        out_shape.append(jax.ShapeDtypeStruct((stat_rows, stat_width), jnp.float32))
    results = pl.pallas_call(
        kernel,
        grid=(pairs,),
        cost_estimate=cost,
        in_specs=[row_spec] + key_specs + value_specs + extra_specs,
        out_specs=out_specs,
        out_shape=out_shape,
    )(queries, *kv_chunks, *kv_chunks, *extra)
    if rows_out:
        return results[0], results[2]
    return results[0], results[1]


def exchanged(x, mask):
    devices = lax.axis_size("seq")
    return lax.ppermute(x, "seq", [(i, i ^ mask) for i in range(devices)])


def projected(rows, norm_gain, weight):
    normed = layer_norm(rows, norm_gain).astype(jnp.bfloat16)
    return jnp.dot(normed, weight, preferred_element_type=jnp.float32).astype(jnp.bfloat16)


def body(layer_input, norm_gain, projection, output_weight, deep_weight, skip_weight, conv_kernel):
    token_count, model_width = layer_input.shape
    head_size = model_width // HEADS
    score_scale = 1.0 / math.sqrt(head_size)
    half = lax.axis_size("seq") // 2
    queries = projected(layer_input, norm_gain, projection[:, :model_width])
    mirrored_queries = exchanged(queries, half)
    same_core = [layer_input] + [exchanged(layer_input, mask) for mask in range(2, half, 2)]
    mine = jnp.concatenate(same_core, axis=0)
    theirs = exchanged(mine, 1)
    kv_weight = projection[:, model_width:]
    kv_chunks = [projected(mine, norm_gain, kv_weight), projected(theirs, norm_gain, kv_weight)]
    remote_out, remote_lse = attention(
        mirrored_queries, kv_chunks, head_size, score_scale, jnp.bfloat16, False, rows_out=True
    )
    heads = model_width // head_size
    other_out = exchanged(remote_out, half)
    row_major = Layout(major_to_minor=(0, 1))
    sent_lse = with_layout_constraint(remote_lse, row_major)
    other_lse = with_layout_constraint(exchanged(sent_lse, half), row_major)[:heads].T
    own_out, own_rows = attention(
        queries,
        kv_chunks,
        head_size,
        score_scale,
        jnp.float32,
        False,
        after=remote_out,
        rows_out=True,
    )
    own_lse = own_rows[:heads].T
    top = jnp.maximum(own_lse, other_lse) + 0 * other_out[:1, :1].astype(jnp.float32)
    own_weight = jnp.repeat(jnp.exp(own_lse - top), head_size, axis=1)
    other_weight = jnp.repeat(jnp.exp(other_lse - top), head_size, axis=1)
    attended = (
        (own_weight * own_out + other_weight * other_out.astype(jnp.float32))
        / (own_weight + other_weight)
    ).astype(jnp.bfloat16)
    encoded = (
        layer_input.astype(jnp.float32)
        + jnp.dot(attended, output_weight, preferred_element_type=jnp.float32)
    ).astype(jnp.bfloat16)
    position = lax.axis_index("seq")
    half_rows = token_count // GZ
    input_grid = layer_input.reshape(1, half_rows, GZ, model_width)
    encoded_grid = encoded.reshape(1, half_rows, GZ, model_width)
    joined = jnp.concatenate(
        [upsample(encoded_grid, deep_weight), upsample(input_grid, skip_weight)], axis=-1
    )
    lower_half = position % 2 == 0
    boundary = jnp.where(lower_half, joined[:, -1:], joined[:, :1])
    partner = swapped(boundary, "seq", 0)
    zero_plane = jnp.zeros_like(partner)
    low_rim = jnp.where(lower_half, zero_plane, partner)
    high_rim = jnp.where(lower_half, partner, zero_plane)
    extended = jnp.concatenate([low_rim, joined, high_rim], axis=1)
    low_plane = plane_send(extended[-1:], 2)
    high_plane = plane_send(extended[:1], -2)
    decoded = convolve(extended, low_plane, high_plane, conv_kernel)[None]
    return (encoded, decoded)


def solution(mesh):
    return jax.shard_map(
        body,
        mesh=mesh,
        in_specs=(P(("groups", "seq"), None), P(), P(), P(), P(), P(), P()),
        out_specs=(P(("groups", "seq"), None), P(("groups", "seq"), None, None, None, None)),
        check_vma=False,
    )
```

```python
import math

import jax
import jax.numpy as jnp
from jax import lax
from jax.experimental import pallas as pl
from jax.experimental.pallas import tpu as pltpu
from jax.experimental.layout import Layout, with_layout_constraint
from jax.sharding import PartitionSpec as P

HEADS = 12
GZ = 8


epsilon = 1e-06
leak_slope = 0.01


def shifted(block, axis, distance):
    devices = range(lax.axis_size(axis))
    route = [(i - distance, i) for i in devices if i - distance in devices]
    return lax.ppermute(block, axis, route)


def swapped(x, axis, distance):
    return lax.ppermute(x, axis, [(i, i ^ 1 << distance) for i in range(lax.axis_size(axis))])


def layer_norm(inputs, gain):
    values32 = inputs.astype(jnp.float32)
    row_mean = jnp.mean(values32, axis=-1, keepdims=True)
    centered = values32 - row_mean
    row_var = jnp.mean(centered * centered, axis=-1, keepdims=True)
    return centered * lax.rsqrt(row_var + epsilon) * gain.astype(jnp.float32)


def to_voxels(flat_out, channels):
    extent_x, extent_y, extent_z = (flat_out.shape[0], flat_out.shape[1], flat_out.shape[2])
    shaped = flat_out.reshape(extent_x, extent_y, extent_z, 2, 2, 2, channels)
    shaped = shaped.transpose(0, 3, 1, 4, 2, 5, 6)
    return shaped.reshape(2 * extent_x, 2 * extent_y, 2 * extent_z, channels)


def upsample(token_grid, weight):
    model_width = token_grid.shape[-1]
    product = jnp.dot(
        token_grid.reshape(-1, model_width), weight, preferred_element_type=jnp.float32
    )
    flat_out = product.astype(jnp.bfloat16).reshape(token_grid.shape[:3] + (weight.shape[1],))
    return to_voxels(flat_out, weight.shape[1] // 8)


def convolve(extended, low_plane, high_plane, conv_kernel):
    def conv(field, kernel, x_pad):
        return lax.conv_general_dilated(
            field[None],
            kernel,
            window_strides=(1, 1, 1),
            padding=((x_pad, x_pad), (0, 0), (1, 1)),
            dimension_numbers=("NDHWC", "DHWIO", "NDHWC"),
            preferred_element_type=jnp.float32,
        )[0]

    interior = lax.optimization_barrier(conv(extended, conv_kernel, 1))
    rims = jnp.concatenate(
        [conv(low_plane, conv_kernel[:1], 0), conv(high_plane, conv_kernel[2:], 0)], axis=0
    )
    accumulated = interior + rims
    activated = jnp.where(accumulated > 0, accumulated, leak_slope * accumulated)
    return activated.astype(jnp.bfloat16)


def plane_send(plane, offset):
    return shifted(plane, "seq", offset)


def attention_kernel(*refs, head_size, score_scale, chunks, whole_output, ordered, rows_out):
    rows_ref = None
    if rows_out:
        rows_ref = refs[-1]
        refs = refs[:-1]
    if ordered:
        refs = refs[:-3] + refs[-2:]
    q_ref = refs[0]
    k_refs = refs[1 : 1 + chunks]
    v_refs = refs[1 + chunks : 1 + 2 * chunks]
    o_ref, lse_ref = refs[-2:]
    step = pl.program_id(0)
    pair = q_ref.shape[-1]
    lane = lax.broadcasted_iota(jnp.int32, (1, pair), 1)
    stat_lane = lax.broadcasted_iota(jnp.int32, (1, lse_ref.shape[-1]), 1)

    @pl.when(step == 0)
    def _():
        lse_ref[...] = jnp.zeros_like(lse_ref)

    q = q_ref[...]
    result = None
    log_sum = lse_ref[...]
    heads = pair // head_size
    for h in range(heads):
        in_head = (lane >= h * head_size) & (lane < (h + 1) * head_size)
        q_h = jnp.where(in_head, q, jnp.zeros_like(q))
        scores = [
            lax.dot_general(
                q_h, k_ref[...], (((1,), (1,)), ((), ())), preferred_element_type=jnp.float32
            )
            for k_ref in k_refs
        ]
        raw_max = scores[0].max(axis=-1, keepdims=True)
        for block in scores[1:]:
            raw_max = jnp.maximum(raw_max, block.max(axis=-1, keepdims=True))
        row_max = raw_max * score_scale
        denominator = None
        numerator = None
        for block, v_ref in zip(scores, v_refs):
            exp_scores = jnp.exp2((block - raw_max) * (score_scale * math.log2(math.e)))
            part_sum = jnp.sum(exp_scores, axis=-1, keepdims=True)
            part = jnp.dot(
                exp_scores.astype(jnp.bfloat16), v_ref[...], preferred_element_type=jnp.float32
            )
            denominator = part_sum if denominator is None else denominator + part_sum
            numerator = part if numerator is None else numerator + part
        head_out = numerator / denominator
        head_lse = row_max + jnp.log(denominator)
        result = head_out if result is None else jnp.where(in_head, head_out, result)
        log_sum = jnp.where(stat_lane == step * heads + h, head_lse, log_sum)
    if whole_output:
        o_ref[:, pl.ds(pl.multiple_of(step * pair, pair), pair)] = result.astype(o_ref.dtype)
    else:
        o_ref[...] = result.astype(o_ref.dtype)
    lse_ref[...] = log_sum
    if rows_out:

        @pl.when(step == pl.num_programs(0) - 1)
        def _():
            rows_ref[...] = jnp.transpose(log_sum)[: rows_ref.shape[0]]


def attention(
    queries, kv_chunks, head_size, score_scale, out_dtype, whole_output, after=None, rows_out=False
):
    token_count, model_width = queries.shape
    pair = 2 * head_size
    pairs = model_width // pair
    chunks = len(kv_chunks)
    kernel = lambda *refs: attention_kernel(
        *refs,
        head_size=head_size,
        score_scale=score_scale,
        chunks=chunks,
        whole_output=whole_output,
        ordered=after is not None,
        rows_out=rows_out,
    )
    key_specs = [pl.BlockSpec((c.shape[0], pair), lambda j: (0, j)) for c in kv_chunks]
    value_specs = [pl.BlockSpec((c.shape[0], pair), lambda j: (0, j + pairs)) for c in kv_chunks]
    row_spec = pl.BlockSpec((token_count, pair), lambda j: (0, j))
    stat_width = 128
    if whole_output:
        out_specs = [
            pl.BlockSpec(memory_space=pltpu.VMEM),
            pl.BlockSpec(memory_space=pltpu.VMEM),
        ]
    else:
        out_specs = [row_spec, pl.BlockSpec((token_count, stat_width), lambda j: (0, 0))]
    extra = [] if after is None else [after]
    extra_specs = [pl.BlockSpec(memory_space=pl.ANY) for _ in extra]
    keys = sum(c.shape[0] for c in kv_chunks)
    cost = pl.CostEstimate(
        flops=8 * token_count * keys * model_width,
        transcendentals=token_count * keys * (model_width // head_size),
        bytes_accessed=2 * keys * 2 * model_width + 8 * token_count * model_width,
    )
    heads = model_width // head_size
    stat_rows = -(-heads // 8) * 8
    if rows_out:
        out_specs = out_specs + [pl.BlockSpec((stat_rows, stat_width), lambda j: (0, 0))]
    out_shape = [
        jax.ShapeDtypeStruct((token_count, model_width), out_dtype),
        jax.ShapeDtypeStruct((token_count, stat_width), jnp.float32),
    ]
    if rows_out:
        out_shape.append(jax.ShapeDtypeStruct((stat_rows, stat_width), jnp.float32))
    results = pl.pallas_call(
        kernel,
        grid=(pairs,),
        cost_estimate=cost,
        in_specs=[row_spec] + key_specs + value_specs + extra_specs,
        out_specs=out_specs,
        out_shape=out_shape,
    )(queries, *kv_chunks, *kv_chunks, *extra)
    if rows_out:
        return results[0], results[2]
    return results[0], results[1]


def exchanged(x, mask):
    devices = lax.axis_size("seq")
    return lax.ppermute(x, "seq", [(i, i ^ mask) for i in range(devices)])


def projected(rows, norm_gain, weight):
    normed = layer_norm(rows, norm_gain).astype(jnp.bfloat16)
    return jnp.dot(normed, weight, preferred_element_type=jnp.float32).astype(jnp.bfloat16)


def body(layer_input, norm_gain, projection, output_weight, deep_weight, skip_weight, conv_kernel):
    token_count, model_width = layer_input.shape
    head_size = model_width // HEADS
    score_scale = 1.0 / math.sqrt(head_size)
    half = lax.axis_size("seq") // 2
    query_weight = projection[:, :model_width]
    mirrored_queries = projected(exchanged(layer_input, half), norm_gain, query_weight)
    queries = projected(layer_input, norm_gain, query_weight)
    same_core = [layer_input] + [exchanged(layer_input, mask) for mask in range(2, half, 2)]
    mine = jnp.concatenate(same_core, axis=0)
    theirs = exchanged(mine, 1)
    kv_weight = projection[:, model_width:]
    kv_chunks = [projected(mine, norm_gain, kv_weight), projected(theirs, norm_gain, kv_weight)]
    remote_out, remote_lse = attention(
        mirrored_queries, kv_chunks, head_size, score_scale, jnp.bfloat16, False, rows_out=True
    )
    heads = model_width // head_size
    other_out = exchanged(remote_out, half)
    row_major = Layout(major_to_minor=(0, 1))
    sent_lse = with_layout_constraint(remote_lse, row_major)
    other_lse = with_layout_constraint(exchanged(sent_lse, half), row_major)[:heads].T
    own_out, own_rows = attention(
        queries,
        kv_chunks,
        head_size,
        score_scale,
        jnp.float32,
        False,
        after=remote_out,
        rows_out=True,
    )
    own_lse = own_rows[:heads].T
    top = jnp.maximum(own_lse, other_lse) + 0 * other_out[:1, :1].astype(jnp.float32)
    own_weight = jnp.repeat(jnp.exp(own_lse - top), head_size, axis=1)
    other_weight = jnp.repeat(jnp.exp(other_lse - top), head_size, axis=1)
    attended = (
        (own_weight * own_out + other_weight * other_out.astype(jnp.float32))
        / (own_weight + other_weight)
    ).astype(jnp.bfloat16)
    encoded = (
        layer_input.astype(jnp.float32)
        + jnp.dot(attended, output_weight, preferred_element_type=jnp.float32)
    ).astype(jnp.bfloat16)
    position = lax.axis_index("seq")
    half_rows = token_count // GZ
    input_grid = layer_input.reshape(1, half_rows, GZ, model_width)
    encoded_grid = encoded.reshape(1, half_rows, GZ, model_width)
    joined = jnp.concatenate(
        [upsample(encoded_grid, deep_weight), upsample(input_grid, skip_weight)], axis=-1
    )
    lower_half = position % 2 == 0
    boundary = jnp.where(lower_half, joined[:, -1:], joined[:, :1])
    partner = swapped(boundary, "seq", 0)
    zero_plane = jnp.zeros_like(partner)
    low_rim = jnp.where(lower_half, zero_plane, partner)
    high_rim = jnp.where(lower_half, partner, zero_plane)
    extended = jnp.concatenate([low_rim, joined, high_rim], axis=1)
    low_plane = plane_send(extended[-1:], 2)
    high_plane = plane_send(extended[:1], -2)
    decoded = convolve(extended, low_plane, high_plane, conv_kernel)[None]
    return (encoded, decoded)


def solution(mesh):
    return jax.shard_map(
        body,
        mesh=mesh,
        in_specs=(P(("groups", "seq"), None), P(), P(), P(), P(), P(), P()),
        out_specs=(P(("groups", "seq"), None), P(("groups", "seq"), None, None, None, None)),
        check_vma=False,
    )
```

```python
import math

import jax
import jax.numpy as jnp
from jax import lax
from jax.experimental import pallas as pl
from jax.experimental.pallas import tpu as pltpu
from jax.experimental.layout import Layout, with_layout_constraint
from jax.sharding import PartitionSpec as P

HEADS = 12
GZ = 8


epsilon = 1e-06
leak_slope = 0.01


def shifted(block, axis, distance):
    devices = range(lax.axis_size(axis))
    route = [(i - distance, i) for i in devices if i - distance in devices]
    return lax.ppermute(block, axis, route)


def swapped(x, axis, distance):
    return lax.ppermute(x, axis, [(i, i ^ 1 << distance) for i in range(lax.axis_size(axis))])


def layer_norm(inputs, gain):
    values32 = inputs.astype(jnp.float32)
    row_mean = jnp.mean(values32, axis=-1, keepdims=True)
    centered = values32 - row_mean
    row_var = jnp.mean(centered * centered, axis=-1, keepdims=True)
    return centered * lax.rsqrt(row_var + epsilon) * gain.astype(jnp.float32)


def to_voxels(flat_out, channels):
    extent_x, extent_y, extent_z = (flat_out.shape[0], flat_out.shape[1], flat_out.shape[2])
    shaped = flat_out.reshape(extent_x, extent_y, extent_z, 2, 2, 2, channels)
    shaped = shaped.transpose(0, 3, 1, 4, 2, 5, 6)
    return shaped.reshape(2 * extent_x, 2 * extent_y, 2 * extent_z, channels)


def upsample(token_grid, weight):
    model_width = token_grid.shape[-1]
    product = jnp.dot(
        token_grid.reshape(-1, model_width), weight, preferred_element_type=jnp.float32
    )
    flat_out = product.astype(jnp.bfloat16).reshape(token_grid.shape[:3] + (weight.shape[1],))
    return to_voxels(flat_out, weight.shape[1] // 8)


def convolve(extended, low_plane, high_plane, conv_kernel):
    def conv(field, kernel, x_pad):
        return lax.conv_general_dilated(
            field.transpose(0, 2, 1, 3)[None],
            kernel.transpose(0, 2, 1, 3, 4),
            window_strides=(1, 1, 1),
            padding=((x_pad, x_pad), (1, 1), (0, 0)),
            dimension_numbers=("NDHWC", "DHWIO", "NDHWC"),
            preferred_element_type=jnp.float32,
        )[0].transpose(0, 2, 1, 3)

    interior = lax.optimization_barrier(conv(extended, conv_kernel, 1))
    rims = jnp.concatenate(
        [conv(low_plane, conv_kernel[:1], 0), conv(high_plane, conv_kernel[2:], 0)], axis=0
    )
    accumulated = interior + rims
    activated = jnp.where(accumulated > 0, accumulated, leak_slope * accumulated)
    return activated.astype(jnp.bfloat16)


def plane_send(plane, offset):
    return shifted(plane, "seq", offset)


def attention_kernel(*refs, head_size, score_scale, chunks, whole_output, ordered, rows_out):
    rows_ref = None
    if rows_out:
        rows_ref = refs[-1]
        refs = refs[:-1]
    if ordered:
        refs = refs[:-3] + refs[-2:]
    q_ref = refs[0]
    k_refs = refs[1 : 1 + chunks]
    v_refs = refs[1 + chunks : 1 + 2 * chunks]
    o_ref, lse_ref = refs[-2:]
    step = pl.program_id(0)
    pair = q_ref.shape[-1]
    lane = lax.broadcasted_iota(jnp.int32, (1, pair), 1)
    stat_lane = lax.broadcasted_iota(jnp.int32, (1, lse_ref.shape[-1]), 1)

    @pl.when(step == 0)
    def _():
        lse_ref[...] = jnp.zeros_like(lse_ref)

    q = q_ref[...]
    result = None
    log_sum = lse_ref[...]
    heads = pair // head_size
    for h in range(heads):
        in_head = (lane >= h * head_size) & (lane < (h + 1) * head_size)
        q_h = jnp.where(in_head, q, jnp.zeros_like(q))
        scores = [
            lax.dot_general(
                q_h, k_ref[...], (((1,), (1,)), ((), ())), preferred_element_type=jnp.float32
            )
            for k_ref in k_refs
        ]
        raw_max = scores[0].max(axis=-1, keepdims=True)
        for block in scores[1:]:
            raw_max = jnp.maximum(raw_max, block.max(axis=-1, keepdims=True))
        row_max = raw_max * score_scale
        denominator = None
        numerator = None
        for block, v_ref in zip(scores, v_refs):
            exp_scores = jnp.exp2((block - raw_max) * (score_scale * math.log2(math.e)))
            part_sum = jnp.sum(exp_scores, axis=-1, keepdims=True)
            part = jnp.dot(
                exp_scores.astype(jnp.bfloat16), v_ref[...], preferred_element_type=jnp.float32
            )
            denominator = part_sum if denominator is None else denominator + part_sum
            numerator = part if numerator is None else numerator + part
        head_out = numerator / denominator
        head_lse = row_max + jnp.log(denominator)
        result = head_out if result is None else jnp.where(in_head, head_out, result)
        log_sum = jnp.where(stat_lane == step * heads + h, head_lse, log_sum)
    if whole_output:
        o_ref[:, pl.ds(pl.multiple_of(step * pair, pair), pair)] = result.astype(o_ref.dtype)
    else:
        o_ref[...] = result.astype(o_ref.dtype)
    lse_ref[...] = log_sum
    if rows_out:

        @pl.when(step == pl.num_programs(0) - 1)
        def _():
            rows_ref[...] = jnp.transpose(log_sum)[: rows_ref.shape[0]]


def attention(
    queries, kv_chunks, head_size, score_scale, out_dtype, whole_output, after=None, rows_out=False
):
    token_count, model_width = queries.shape
    pair = 2 * head_size
    pairs = model_width // pair
    chunks = len(kv_chunks)
    kernel = lambda *refs: attention_kernel(
        *refs,
        head_size=head_size,
        score_scale=score_scale,
        chunks=chunks,
        whole_output=whole_output,
        ordered=after is not None,
        rows_out=rows_out,
    )
    key_specs = [pl.BlockSpec((c.shape[0], pair), lambda j: (0, j)) for c in kv_chunks]
    value_specs = [pl.BlockSpec((c.shape[0], pair), lambda j: (0, j + pairs)) for c in kv_chunks]
    row_spec = pl.BlockSpec((token_count, pair), lambda j: (0, j))
    stat_width = 128
    if whole_output:
        out_specs = [
            pl.BlockSpec(memory_space=pltpu.VMEM),
            pl.BlockSpec(memory_space=pltpu.VMEM),
        ]
    else:
        out_specs = [row_spec, pl.BlockSpec((token_count, stat_width), lambda j: (0, 0))]
    extra = [] if after is None else [after]
    extra_specs = [pl.BlockSpec(memory_space=pl.ANY) for _ in extra]
    keys = sum(c.shape[0] for c in kv_chunks)
    cost = pl.CostEstimate(
        flops=8 * token_count * keys * model_width,
        transcendentals=token_count * keys * (model_width // head_size),
        bytes_accessed=2 * keys * 2 * model_width + 8 * token_count * model_width,
    )
    heads = model_width // head_size
    stat_rows = -(-heads // 8) * 8
    if rows_out:
        out_specs = out_specs + [pl.BlockSpec((stat_rows, stat_width), lambda j: (0, 0))]
    out_shape = [
        jax.ShapeDtypeStruct((token_count, model_width), out_dtype),
        jax.ShapeDtypeStruct((token_count, stat_width), jnp.float32),
    ]
    if rows_out:
        out_shape.append(jax.ShapeDtypeStruct((stat_rows, stat_width), jnp.float32))
    results = pl.pallas_call(
        kernel,
        grid=(pairs,),
        cost_estimate=cost,
        in_specs=[row_spec] + key_specs + value_specs + extra_specs,
        out_specs=out_specs,
        out_shape=out_shape,
    )(queries, *kv_chunks, *kv_chunks, *extra)
    if rows_out:
        return results[0], results[2]
    return results[0], results[1]


def exchanged(x, mask):
    devices = lax.axis_size("seq")
    return lax.ppermute(x, "seq", [(i, i ^ mask) for i in range(devices)])


def projected(rows, norm_gain, weight):
    normed = layer_norm(rows, norm_gain).astype(jnp.bfloat16)
    return jnp.dot(normed, weight, preferred_element_type=jnp.float32).astype(jnp.bfloat16)


def body(layer_input, norm_gain, projection, output_weight, deep_weight, skip_weight, conv_kernel):
    token_count, model_width = layer_input.shape
    head_size = model_width // HEADS
    score_scale = 1.0 / math.sqrt(head_size)
    half = lax.axis_size("seq") // 2
    queries = projected(layer_input, norm_gain, projection[:, :model_width])
    mirrored_queries = exchanged(queries, half)
    same_core = [layer_input] + [exchanged(layer_input, mask) for mask in range(2, half, 2)]
    mine = jnp.concatenate(same_core, axis=0)
    theirs = exchanged(mine, 1)
    kv_weight = projection[:, model_width:]
    kv_chunks = [projected(mine, norm_gain, kv_weight), projected(theirs, norm_gain, kv_weight)]
    remote_out, remote_lse = attention(
        mirrored_queries, kv_chunks, head_size, score_scale, jnp.bfloat16, False, rows_out=True
    )
    heads = model_width // head_size
    other_out = exchanged(remote_out, half)
    row_major = Layout(major_to_minor=(0, 1))
    sent_lse = with_layout_constraint(remote_lse, row_major)
    other_lse = with_layout_constraint(exchanged(sent_lse, half), row_major)[:heads].T
    own_out, own_lse = attention(
        queries, kv_chunks, head_size, score_scale, jnp.float32, False, after=remote_out
    )
    own_lse = own_lse[:, :heads]
    top = jnp.maximum(own_lse, other_lse) + 0 * other_out[:1, :1].astype(jnp.float32)
    own_weight = jnp.repeat(jnp.exp(own_lse - top), head_size, axis=1)
    other_weight = jnp.repeat(jnp.exp(other_lse - top), head_size, axis=1)
    attended = (
        (own_weight * own_out + other_weight * other_out.astype(jnp.float32))
        / (own_weight + other_weight)
    ).astype(jnp.bfloat16)
    encoded = (
        layer_input.astype(jnp.float32)
        + jnp.dot(attended, output_weight, preferred_element_type=jnp.float32)
    ).astype(jnp.bfloat16)
    position = lax.axis_index("seq")
    half_rows = token_count // GZ
    input_grid = layer_input.reshape(1, half_rows, GZ, model_width)
    encoded_grid = encoded.reshape(1, half_rows, GZ, model_width)
    joined = jnp.concatenate(
        [upsample(encoded_grid, deep_weight), upsample(input_grid, skip_weight)], axis=-1
    )
    lower_half = position % 2 == 0
    boundary = jnp.where(lower_half, joined[:, -1:], joined[:, :1])
    partner = swapped(boundary, "seq", 0)
    zero_plane = jnp.zeros_like(partner)
    low_rim = jnp.where(lower_half, zero_plane, partner)
    high_rim = jnp.where(lower_half, partner, zero_plane)
    extended = jnp.concatenate([low_rim, joined, high_rim], axis=1)
    low_plane = plane_send(extended[-1:], 2)
    high_plane = plane_send(extended[:1], -2)
    decoded = convolve(extended, low_plane, high_plane, conv_kernel)[None]
    return (encoded, decoded)


def solution(mesh):
    return jax.shard_map(
        body,
        mesh=mesh,
        in_specs=(P(("groups", "seq"), None), P(), P(), P(), P(), P(), P()),
        out_specs=(P(("groups", "seq"), None), P(("groups", "seq"), None, None, None, None)),
        check_vma=False,
    )
```

```python
import math

import jax
import jax.numpy as jnp
from jax import lax
from jax.experimental import pallas as pl
from jax.experimental.pallas import tpu as pltpu
from jax.experimental.layout import Layout, with_layout_constraint
from jax.sharding import PartitionSpec as P

HEADS = 12
GZ = 8


epsilon = 1e-06
leak_slope = 0.01


def shifted(block, axis, distance):
    devices = range(lax.axis_size(axis))
    route = [(i - distance, i) for i in devices if i - distance in devices]
    return lax.ppermute(block, axis, route)


def swapped(x, axis, distance):
    return lax.ppermute(x, axis, [(i, i ^ 1 << distance) for i in range(lax.axis_size(axis))])


def layer_norm(inputs, gain):
    values32 = inputs.astype(jnp.float32)
    row_mean = jnp.mean(values32, axis=-1, keepdims=True)
    centered = values32 - row_mean
    row_var = jnp.mean(centered * centered, axis=-1, keepdims=True)
    return centered * lax.rsqrt(row_var + epsilon) * gain.astype(jnp.float32)


def to_voxels(flat_out, channels):
    extent_x, extent_y, extent_z = (flat_out.shape[0], flat_out.shape[1], flat_out.shape[2])
    shaped = flat_out.reshape(extent_x, extent_y, extent_z, 2, 2, 2, channels)
    shaped = shaped.transpose(0, 3, 1, 4, 2, 5, 6)
    return shaped.reshape(2 * extent_x, 2 * extent_y, 2 * extent_z, channels)


def upsample(token_grid, weight):
    model_width = token_grid.shape[-1]
    product = jnp.dot(
        token_grid.reshape(-1, model_width), weight, preferred_element_type=jnp.float32
    )
    flat_out = product.astype(jnp.bfloat16).reshape(token_grid.shape[:3] + (weight.shape[1],))
    return to_voxels(flat_out, weight.shape[1] // 8)


def convolve(extended, low_plane, high_plane, conv_kernel):
    def conv(field, kernel, x_pad):
        return lax.conv_general_dilated(
            field.transpose(0, 2, 1, 3)[None],
            kernel.transpose(0, 2, 1, 3, 4),
            window_strides=(1, 1, 1),
            padding=((x_pad, x_pad), (1, 1), (0, 0)),
            dimension_numbers=("NDHWC", "DHWIO", "NDHWC"),
            preferred_element_type=jnp.float32,
        )[0].transpose(0, 2, 1, 3)

    interior = lax.optimization_barrier(conv(extended, conv_kernel, 1))
    rims = jnp.concatenate(
        [conv(low_plane, conv_kernel[:1], 0), conv(high_plane, conv_kernel[2:], 0)], axis=0
    )
    accumulated = interior + rims
    activated = jnp.where(accumulated > 0, accumulated, leak_slope * accumulated)
    return activated.astype(jnp.bfloat16)


def plane_send(plane, offset):
    return shifted(plane, "seq", offset)


def attention_kernel(*refs, head_size, score_scale, chunks, whole_output, ordered, rows_out):
    rows_ref = None
    if rows_out:
        rows_ref = refs[-1]
        refs = refs[:-1]
    if ordered:
        refs = refs[:-3] + refs[-2:]
    q_ref = refs[0]
    k_refs = refs[1 : 1 + chunks]
    v_refs = refs[1 + chunks : 1 + 2 * chunks]
    o_ref, lse_ref = refs[-2:]
    step = pl.program_id(0)
    pair = q_ref.shape[-1]
    lane = lax.broadcasted_iota(jnp.int32, (1, pair), 1)
    stat_lane = lax.broadcasted_iota(jnp.int32, (1, lse_ref.shape[-1]), 1)

    @pl.when(step == 0)
    def _():
        lse_ref[...] = jnp.zeros_like(lse_ref)

    q = q_ref[...]
    result = None
    log_sum = lse_ref[...]
    heads = pair // head_size
    for h in range(heads):
        in_head = (lane >= h * head_size) & (lane < (h + 1) * head_size)
        q_h = jnp.where(in_head, q, jnp.zeros_like(q))
        scores = [
            jnp.dot(q_h, k_ref[...], preferred_element_type=jnp.float32)
            for k_ref in k_refs
        ]
        raw_max = scores[0].max(axis=-1, keepdims=True)
        for block in scores[1:]:
            raw_max = jnp.maximum(raw_max, block.max(axis=-1, keepdims=True))
        row_max = raw_max * score_scale
        denominator = None
        numerator = None
        for block, v_ref in zip(scores, v_refs):
            exp_scores = jnp.exp2((block - raw_max) * (score_scale * math.log2(math.e)))
            part_sum = jnp.sum(exp_scores, axis=-1, keepdims=True)
            part = jnp.dot(
                exp_scores.astype(jnp.bfloat16), v_ref[...], preferred_element_type=jnp.float32
            )
            denominator = part_sum if denominator is None else denominator + part_sum
            numerator = part if numerator is None else numerator + part
        head_out = numerator / denominator
        head_lse = row_max + jnp.log(denominator)
        result = head_out if result is None else jnp.where(in_head, head_out, result)
        log_sum = jnp.where(stat_lane == step * heads + h, head_lse, log_sum)
    if whole_output:
        o_ref[:, pl.ds(pl.multiple_of(step * pair, pair), pair)] = result.astype(o_ref.dtype)
    else:
        o_ref[...] = result.astype(o_ref.dtype)
    lse_ref[...] = log_sum
    if rows_out:

        @pl.when(step == pl.num_programs(0) - 1)
        def _():
            rows_ref[...] = jnp.transpose(log_sum)[: rows_ref.shape[0]]


def attention(
    queries, kv_chunks, head_size, score_scale, out_dtype, whole_output, after=None, rows_out=False
):
    token_count, model_width = queries.shape
    pair = 2 * head_size
    pairs = model_width // pair
    chunks = len(kv_chunks)
    kernel = lambda *refs: attention_kernel(
        *refs,
        head_size=head_size,
        score_scale=score_scale,
        chunks=chunks,
        whole_output=whole_output,
        ordered=after is not None,
        rows_out=rows_out,
    )
    key_specs = [pl.BlockSpec((pair, c.shape[1]), lambda j: (j, 0)) for c, _ in kv_chunks]
    value_specs = [pl.BlockSpec((c.shape[0], pair), lambda j: (0, j)) for _, c in kv_chunks]
    row_spec = pl.BlockSpec((token_count, pair), lambda j: (0, j))
    stat_width = 128
    if whole_output:
        out_specs = [
            pl.BlockSpec(memory_space=pltpu.VMEM),
            pl.BlockSpec(memory_space=pltpu.VMEM),
        ]
    else:
        out_specs = [row_spec, pl.BlockSpec((token_count, stat_width), lambda j: (0, 0))]
    extra = [] if after is None else [after]
    extra_specs = [pl.BlockSpec(memory_space=pl.ANY) for _ in extra]
    keys = sum(c.shape[0] for _, c in kv_chunks)
    cost = pl.CostEstimate(
        flops=8 * token_count * keys * model_width,
        transcendentals=token_count * keys * (model_width // head_size),
        bytes_accessed=2 * keys * 2 * model_width + 8 * token_count * model_width,
    )
    heads = model_width // head_size
    stat_rows = -(-heads // 8) * 8
    if rows_out:
        out_specs = out_specs + [pl.BlockSpec((stat_rows, stat_width), lambda j: (0, 0))]
    out_shape = [
        jax.ShapeDtypeStruct((token_count, model_width), out_dtype),
        jax.ShapeDtypeStruct((token_count, stat_width), jnp.float32),
    ]
    if rows_out:
        out_shape.append(jax.ShapeDtypeStruct((stat_rows, stat_width), jnp.float32))
    results = pl.pallas_call(
        kernel,
        grid=(pairs,),
        cost_estimate=cost,
        in_specs=[row_spec] + key_specs + value_specs + extra_specs,
        out_specs=out_specs,
        out_shape=out_shape,
    )(queries, *[k for k, _ in kv_chunks], *[v for _, v in kv_chunks], *extra)
    if rows_out:
        return results[0], results[2]
    return results[0], results[1]


def exchanged(x, mask):
    devices = lax.axis_size("seq")
    return lax.ppermute(x, "seq", [(i, i ^ mask) for i in range(devices)])


def projected(rows, norm_gain, weight):
    normed = layer_norm(rows, norm_gain).astype(jnp.bfloat16)
    return jnp.dot(normed, weight, preferred_element_type=jnp.float32).astype(jnp.bfloat16)


def keys_values(rows, norm_gain, key_weight, value_weight):
    normed = layer_norm(rows, norm_gain).astype(jnp.bfloat16)
    keys_t = lax.dot_general(
        key_weight, normed, (((0,), (1,)), ((), ())), preferred_element_type=jnp.float32
    ).astype(jnp.bfloat16)
    values = jnp.dot(normed, value_weight, preferred_element_type=jnp.float32).astype(jnp.bfloat16)
    return keys_t, values


def body(layer_input, norm_gain, projection, output_weight, deep_weight, skip_weight, conv_kernel):
    token_count, model_width = layer_input.shape
    head_size = model_width // HEADS
    score_scale = 1.0 / math.sqrt(head_size)
    half = lax.axis_size("seq") // 2
    queries = projected(layer_input, norm_gain, projection[:, :model_width])
    mirrored_queries = exchanged(queries, half)
    same_core = [layer_input] + [exchanged(layer_input, mask) for mask in range(2, half, 2)]
    mine = jnp.concatenate(same_core, axis=0)
    theirs = exchanged(mine, 1)
    key_weight = projection[:, model_width : 2 * model_width]
    value_weight = projection[:, 2 * model_width :]
    kv_chunks = [keys_values(rows, norm_gain, key_weight, value_weight) for rows in (mine, theirs)]
    remote_out, remote_lse = attention(
        mirrored_queries, kv_chunks, head_size, score_scale, jnp.bfloat16, False, rows_out=True
    )
    heads = model_width // head_size
    other_out = exchanged(remote_out, half)
    row_major = Layout(major_to_minor=(0, 1))
    sent_lse = with_layout_constraint(remote_lse, row_major)
    other_lse = with_layout_constraint(exchanged(sent_lse, half), row_major)[:heads].T
    own_out, own_lse = attention(
        queries, kv_chunks, head_size, score_scale, jnp.float32, False, after=remote_out
    )
    own_lse = own_lse[:, :heads]
    top = jnp.maximum(own_lse, other_lse) + 0 * other_out[:1, :1].astype(jnp.float32)
    own_weight = jnp.repeat(jnp.exp(own_lse - top), head_size, axis=1)
    other_weight = jnp.repeat(jnp.exp(other_lse - top), head_size, axis=1)
    attended = (
        (own_weight * own_out + other_weight * other_out.astype(jnp.float32))
        / (own_weight + other_weight)
    ).astype(jnp.bfloat16)
    encoded = (
        layer_input.astype(jnp.float32)
        + jnp.dot(attended, output_weight, preferred_element_type=jnp.float32)
    ).astype(jnp.bfloat16)
    position = lax.axis_index("seq")
    half_rows = token_count // GZ
    input_grid = layer_input.reshape(1, half_rows, GZ, model_width)
    encoded_grid = encoded.reshape(1, half_rows, GZ, model_width)
    joined = jnp.concatenate(
        [upsample(encoded_grid, deep_weight), upsample(input_grid, skip_weight)], axis=-1
    )
    lower_half = position % 2 == 0
    boundary = jnp.where(lower_half, joined[:, -1:], joined[:, :1])
    partner = swapped(boundary, "seq", 0)
    zero_plane = jnp.zeros_like(partner)
    low_rim = jnp.where(lower_half, zero_plane, partner)
    high_rim = jnp.where(lower_half, partner, zero_plane)
    extended = jnp.concatenate([low_rim, joined, high_rim], axis=1)
    low_plane = plane_send(extended[-1:], 2)
    high_plane = plane_send(extended[:1], -2)
    decoded = convolve(extended, low_plane, high_plane, conv_kernel)[None]
    return (encoded, decoded)


def solution(mesh):
    return jax.shard_map(
        body,
        mesh=mesh,
        in_specs=(P(("groups", "seq"), None), P(), P(), P(), P(), P(), P()),
        out_specs=(P(("groups", "seq"), None), P(("groups", "seq"), None, None, None, None)),
        check_vma=False,
    )
```

```python
import math

import jax
import jax.numpy as jnp
from jax import lax
from jax.experimental import pallas as pl
from jax.experimental.pallas import tpu as pltpu
from jax.experimental.layout import Layout, with_layout_constraint
from jax.sharding import PartitionSpec as P

HEADS = 12
GZ = 8


epsilon = 1e-06
leak_slope = 0.01


def shifted(block, axis, distance):
    devices = range(lax.axis_size(axis))
    route = [(i - distance, i) for i in devices if i - distance in devices]
    return lax.ppermute(block, axis, route)


def swapped(x, axis, distance):
    return lax.ppermute(x, axis, [(i, i ^ 1 << distance) for i in range(lax.axis_size(axis))])


def layer_norm(inputs, gain):
    values32 = inputs.astype(jnp.float32)
    row_mean = jnp.mean(values32, axis=-1, keepdims=True)
    centered = values32 - row_mean
    row_var = jnp.mean(centered * centered, axis=-1, keepdims=True)
    return centered * lax.rsqrt(row_var + epsilon) * gain.astype(jnp.float32)


def to_voxels(flat_out, channels):
    extent_x, extent_y, extent_z = (flat_out.shape[0], flat_out.shape[1], flat_out.shape[2])
    shaped = flat_out.reshape(extent_x, extent_y, extent_z, 2, 2, 2, channels)
    shaped = shaped.transpose(0, 3, 1, 4, 2, 5, 6)
    return shaped.reshape(2 * extent_x, 2 * extent_y, 2 * extent_z, channels)


def upsample(token_grid, weight):
    model_width = token_grid.shape[-1]
    product = jnp.dot(
        token_grid.reshape(-1, model_width), weight, preferred_element_type=jnp.float32
    )
    flat_out = product.astype(jnp.bfloat16).reshape(token_grid.shape[:3] + (weight.shape[1],))
    return to_voxels(flat_out, weight.shape[1] // 8)


def convolve(extended, low_plane, high_plane, conv_kernel):
    def conv(field, kernel, x_pad):
        return lax.conv_general_dilated(
            field.transpose(0, 2, 1, 3)[None],
            kernel.transpose(0, 2, 1, 3, 4),
            window_strides=(1, 1, 1),
            padding=((x_pad, x_pad), (1, 1), (0, 0)),
            dimension_numbers=("NDHWC", "DHWIO", "NDHWC"),
            preferred_element_type=jnp.float32,
        )[0].transpose(0, 2, 1, 3)

    interior = lax.optimization_barrier(conv(extended, conv_kernel, 1))
    rims = jnp.concatenate(
        [conv(low_plane, conv_kernel[:1], 0), conv(high_plane, conv_kernel[2:], 0)], axis=0
    )
    accumulated = interior + rims
    activated = jnp.where(accumulated > 0, accumulated, leak_slope * accumulated)
    return activated.astype(jnp.bfloat16)


def plane_send(plane, offset):
    return shifted(plane, "seq", offset)


def attention_kernel(*refs, head_size, score_scale, chunks, whole_output, ordered, rows_out):
    rows_ref = None
    if rows_out:
        rows_ref = refs[-1]
        refs = refs[:-1]
    if ordered:
        refs = refs[:-3] + refs[-2:]
    q_ref = refs[0]
    k_refs = refs[1 : 1 + chunks]
    v_refs = refs[1 + chunks : 1 + 2 * chunks]
    o_ref, lse_ref = refs[-2:]
    step = pl.program_id(0)
    pair = q_ref.shape[-1]
    lane = lax.broadcasted_iota(jnp.int32, (1, pair), 1)
    stat_lane = lax.broadcasted_iota(jnp.int32, (1, lse_ref.shape[-1]), 1)

    @pl.when(step == 0)
    def _():
        lse_ref[...] = jnp.zeros_like(lse_ref)

    q = q_ref[...]
    result = None
    log_sum = lse_ref[...]
    heads = pair // head_size
    for h in range(heads):
        in_head = (lane >= h * head_size) & (lane < (h + 1) * head_size)
        q_h = jnp.where(in_head, q, jnp.zeros_like(q))
        scores = [
            lax.dot_general(
                q_h, k_ref[...], (((1,), (1,)), ((), ())), preferred_element_type=jnp.float32
            )
            for k_ref in k_refs
        ]
        raw_max = scores[0].max(axis=-1, keepdims=True)
        for block in scores[1:]:
            raw_max = jnp.maximum(raw_max, block.max(axis=-1, keepdims=True))
        row_max = raw_max * score_scale
        denominator = None
        numerator = None
        for block, v_ref in zip(scores, v_refs):
            exp_scores = jnp.exp2((block - raw_max) * (score_scale * math.log2(math.e)))
            part_sum = jnp.sum(exp_scores, axis=-1, keepdims=True)
            part = jnp.dot(
                exp_scores.astype(jnp.bfloat16), v_ref[...], preferred_element_type=jnp.float32
            )
            denominator = part_sum if denominator is None else denominator + part_sum
            numerator = part if numerator is None else numerator + part
        head_out = numerator / denominator
        head_lse = row_max + jnp.log(denominator)
        result = head_out if result is None else jnp.where(in_head, head_out, result)
        log_sum = jnp.where(stat_lane == step * heads + h, head_lse, log_sum)
    if whole_output:
        o_ref[:, pl.ds(pl.multiple_of(step * pair, pair), pair)] = result.astype(o_ref.dtype)
    else:
        o_ref[...] = result.astype(o_ref.dtype)
    lse_ref[...] = log_sum
    if rows_out:

        @pl.when(step == pl.num_programs(0) - 1)
        def _():
            rows_ref[...] = jnp.transpose(log_sum)[: rows_ref.shape[0]]


def attention(
    queries, kv_chunks, head_size, score_scale, out_dtype, whole_output, after=None, rows_out=False
):
    token_count, model_width = queries.shape
    pair = 2 * head_size
    pairs = model_width // pair
    chunks = len(kv_chunks)
    kernel = lambda *refs: attention_kernel(
        *refs,
        head_size=head_size,
        score_scale=score_scale,
        chunks=chunks,
        whole_output=whole_output,
        ordered=after is not None,
        rows_out=rows_out,
    )
    key_specs = [pl.BlockSpec((c.shape[0], pair), lambda j: (0, j)) for c in kv_chunks]
    value_specs = [pl.BlockSpec((c.shape[0], pair), lambda j: (0, j + pairs)) for c in kv_chunks]
    row_spec = pl.BlockSpec((token_count, pair), lambda j: (0, j))
    stat_width = 128
    if whole_output:
        out_specs = [
            pl.BlockSpec(memory_space=pltpu.VMEM),
            pl.BlockSpec(memory_space=pltpu.VMEM),
        ]
    else:
        out_specs = [row_spec, pl.BlockSpec((token_count, stat_width), lambda j: (0, 0))]
    extra = [] if after is None else [after]
    extra_specs = [pl.BlockSpec(memory_space=pl.ANY) for _ in extra]
    keys = sum(c.shape[0] for c in kv_chunks)
    cost = pl.CostEstimate(
        flops=8 * token_count * keys * model_width,
        transcendentals=token_count * keys * (model_width // head_size),
        bytes_accessed=2 * keys * 2 * model_width + 8 * token_count * model_width,
    )
    heads = model_width // head_size
    stat_rows = -(-heads // 8) * 8
    if rows_out:
        out_specs = out_specs + [pl.BlockSpec((stat_rows, stat_width), lambda j: (0, 0))]
    out_shape = [
        jax.ShapeDtypeStruct((token_count, model_width), out_dtype),
        jax.ShapeDtypeStruct((token_count, stat_width), jnp.float32),
    ]
    if rows_out:
        out_shape.append(jax.ShapeDtypeStruct((stat_rows, stat_width), jnp.float32))
    results = pl.pallas_call(
        kernel,
        grid=(pairs,),
        cost_estimate=cost,
        in_specs=[row_spec] + key_specs + value_specs + extra_specs,
        out_specs=out_specs,
        out_shape=out_shape,
    )(queries, *kv_chunks, *kv_chunks, *extra)
    if rows_out:
        return results[0], results[2]
    return results[0], results[1]


def exchanged(x, mask):
    devices = lax.axis_size("seq")
    return lax.ppermute(x, "seq", [(i, i ^ mask) for i in range(devices)])


def projected(rows, norm_gain, weight):
    normed = layer_norm(rows, norm_gain).astype(jnp.bfloat16)
    return jnp.dot(normed, weight, preferred_element_type=jnp.float32).astype(jnp.bfloat16)


def body(layer_input, norm_gain, projection, output_weight, deep_weight, skip_weight, conv_kernel):
    token_count, model_width = layer_input.shape
    head_size = model_width // HEADS
    score_scale = 1.0 / math.sqrt(head_size)
    half = lax.axis_size("seq") // 2
    queries = projected(layer_input, norm_gain, projection[:, :model_width])
    mirrored_queries = exchanged(queries, half)
    same_core = [layer_input] + [exchanged(layer_input, mask) for mask in range(2, half, 2)]
    mine = jnp.concatenate(same_core, axis=0)
    theirs = exchanged(mine, 1)
    kv_weight = projection[:, model_width:]
    kv_chunks = [projected(mine, norm_gain, kv_weight), projected(theirs, norm_gain, kv_weight)]
    remote_out, remote_lse = attention(
        mirrored_queries, kv_chunks, head_size, score_scale, jnp.bfloat16, False, rows_out=True
    )
    heads = model_width // head_size
    other_out = exchanged(remote_out, half)
    row_major = Layout(major_to_minor=(0, 1))
    sent_lse = with_layout_constraint(remote_lse, row_major)
    other_lse = with_layout_constraint(exchanged(sent_lse, half), row_major)[:heads].T
    own_out, own_rows = attention(
        queries,
        kv_chunks,
        head_size,
        score_scale,
        jnp.float32,
        False,
        after=remote_out,
        rows_out=True,
    )
    own_lse = own_rows[:heads].T
    top = jnp.maximum(own_lse, other_lse) + 0 * other_out[:1, :1].astype(jnp.float32)
    own_weight = jnp.repeat(jnp.exp(own_lse - top), head_size, axis=1)
    other_weight = jnp.repeat(jnp.exp(other_lse - top), head_size, axis=1)
    attended = (
        (own_weight * own_out + other_weight * other_out.astype(jnp.float32))
        / (own_weight + other_weight)
    ).astype(jnp.bfloat16)
    encoded = (
        layer_input.astype(jnp.float32)
        + jnp.dot(attended, output_weight, preferred_element_type=jnp.float32)
    ).astype(jnp.bfloat16)
    position = lax.axis_index("seq")
    half_rows = token_count // GZ
    input_grid = layer_input.reshape(1, half_rows, GZ, model_width)
    encoded_grid = encoded.reshape(1, half_rows, GZ, model_width)
    joined = jnp.concatenate(
        [upsample(encoded_grid, deep_weight), upsample(input_grid, skip_weight)], axis=-1
    )
    lower_half = position % 2 == 0
    boundary = jnp.where(lower_half, joined[:, -1:], joined[:, :1])
    partner = swapped(boundary, "seq", 0)
    zero_plane = jnp.zeros_like(partner)
    low_rim = jnp.where(lower_half, zero_plane, partner)
    high_rim = jnp.where(lower_half, partner, zero_plane)
    extended = jnp.concatenate([low_rim, joined, high_rim], axis=1)
    low_plane = plane_send(extended[-1:], 2)
    high_plane = plane_send(extended[:1], -2)
    decoded = convolve(extended, low_plane, high_plane, conv_kernel)[None]
    return (encoded, decoded)


def solution(mesh):
    return jax.shard_map(
        body,
        mesh=mesh,
        in_specs=(P(("groups", "seq"), None), P(), P(), P(), P(), P(), P()),
        out_specs=(P(("groups", "seq"), None), P(("groups", "seq"), None, None, None, None)),
        check_vma=False,
    )
```

```python
import math

import jax
import jax.numpy as jnp
from jax import lax
from jax.experimental import pallas as pl
from jax.experimental.pallas import tpu as pltpu
from jax.experimental.layout import Layout, with_layout_constraint
from jax.sharding import PartitionSpec as P

HEADS = 12
GZ = 8


epsilon = 1e-06
leak_slope = 0.01


def shifted(block, axis, distance):
    devices = range(lax.axis_size(axis))
    route = [(i - distance, i) for i in devices if i - distance in devices]
    return lax.ppermute(block, axis, route)


def swapped(x, axis, distance):
    return lax.ppermute(x, axis, [(i, i ^ 1 << distance) for i in range(lax.axis_size(axis))])


def layer_norm(inputs, gain):
    values32 = inputs.astype(jnp.float32)
    row_mean = jnp.mean(values32, axis=-1, keepdims=True)
    centered = values32 - row_mean
    row_var = jnp.mean(centered * centered, axis=-1, keepdims=True)
    return centered * lax.rsqrt(row_var + epsilon) * gain.astype(jnp.float32)


def to_voxels(flat_out, channels):
    extent_x, extent_y, extent_z = (flat_out.shape[0], flat_out.shape[1], flat_out.shape[2])
    shaped = flat_out.reshape(extent_x, extent_y, extent_z, 2, 2, 2, channels)
    shaped = shaped.transpose(0, 3, 1, 4, 2, 5, 6)
    return shaped.reshape(2 * extent_x, 2 * extent_y, 2 * extent_z, channels)


def upsample(token_grid, weight):
    model_width = token_grid.shape[-1]
    product = jnp.dot(
        token_grid.reshape(-1, model_width), weight, preferred_element_type=jnp.float32
    )
    flat_out = product.astype(jnp.bfloat16).reshape(token_grid.shape[:3] + (weight.shape[1],))
    return to_voxels(flat_out, weight.shape[1] // 8)


def convolve(extended, low_plane, high_plane, conv_kernel):
    def conv(field, kernel, x_pad):
        return lax.conv_general_dilated(
            field.transpose(0, 2, 1, 3)[None],
            kernel.transpose(0, 2, 1, 3, 4),
            window_strides=(1, 1, 1),
            padding=((x_pad, x_pad), (1, 1), (0, 0)),
            dimension_numbers=("NDHWC", "DHWIO", "NDHWC"),
            preferred_element_type=jnp.float32,
        )[0].transpose(0, 2, 1, 3)

    interior = lax.optimization_barrier(conv(extended, conv_kernel, 1))
    rims = jnp.concatenate(
        [conv(low_plane, conv_kernel[:1], 0), conv(high_plane, conv_kernel[2:], 0)], axis=0
    )
    accumulated = interior + rims
    activated = jnp.where(accumulated > 0, accumulated, leak_slope * accumulated)
    return activated.astype(jnp.bfloat16)


def plane_send(plane, offset):
    return shifted(plane, "seq", offset)


def attention_kernel(*refs, head_size, score_scale, chunks, whole_output, ordered, rows_out):
    rows_ref = None
    if rows_out:
        rows_ref = refs[-1]
        refs = refs[:-1]
    if ordered:
        refs = refs[:-3] + refs[-2:]
    q_ref = refs[0]
    k_refs = refs[1 : 1 + chunks]
    v_refs = refs[1 + chunks : 1 + 2 * chunks]
    o_ref, lse_ref = refs[-2:]
    step = pl.program_id(0)
    pair = q_ref.shape[-1]
    lane = lax.broadcasted_iota(jnp.int32, (1, pair), 1)
    stat_lane = lax.broadcasted_iota(jnp.int32, (1, lse_ref.shape[-1]), 1)

    @pl.when(step == 0)
    def _():
        lse_ref[...] = jnp.zeros_like(lse_ref)

    q = q_ref[...]
    result = None
    log_sum = lse_ref[...]
    heads = pair // head_size
    for h in range(heads):
        in_head = (lane >= h * head_size) & (lane < (h + 1) * head_size)
        q_h = jnp.where(in_head, q, jnp.zeros_like(q))
        scores = [
            lax.dot_general(
                q_h, k_ref[...], (((1,), (1,)), ((), ())), preferred_element_type=jnp.float32
            )
            for k_ref in k_refs
        ]
        raw_max = scores[0].max(axis=-1, keepdims=True)
        for block in scores[1:]:
            raw_max = jnp.maximum(raw_max, block.max(axis=-1, keepdims=True))
        row_max = raw_max * score_scale
        denominator = None
        numerator = None
        for block, v_ref in zip(scores, v_refs):
            exp_scores = jnp.exp2((block - raw_max) * (score_scale * math.log2(math.e)))
            part_sum = jnp.sum(exp_scores, axis=-1, keepdims=True)
            part = jnp.dot(
                exp_scores.astype(jnp.bfloat16), v_ref[...], preferred_element_type=jnp.float32
            )
            denominator = part_sum if denominator is None else denominator + part_sum
            numerator = part if numerator is None else numerator + part
        head_out = numerator / denominator
        head_lse = row_max + jnp.log(denominator)
        result = head_out if result is None else jnp.where(in_head, head_out, result)
        log_sum = jnp.where(stat_lane == step * heads + h, head_lse, log_sum)
    if whole_output:
        o_ref[:, pl.ds(pl.multiple_of(step * pair, pair), pair)] = result.astype(o_ref.dtype)
    else:
        o_ref[...] = result.astype(o_ref.dtype)
    lse_ref[...] = log_sum
    if rows_out:

        @pl.when(step == pl.num_programs(0) - 1)
        def _():
            rows_ref[...] = jnp.transpose(log_sum)[: rows_ref.shape[0]]


def attention(
    queries, kv_chunks, head_size, score_scale, out_dtype, whole_output, after=None, rows_out=False
):
    token_count, model_width = queries.shape
    pair = 2 * head_size
    pairs = model_width // pair
    chunks = len(kv_chunks)
    kernel = lambda *refs: attention_kernel(
        *refs,
        head_size=head_size,
        score_scale=score_scale,
        chunks=chunks,
        whole_output=whole_output,
        ordered=after is not None,
        rows_out=rows_out,
    )
    key_specs = [pl.BlockSpec((c.shape[0], pair), lambda j: (0, j)) for c in kv_chunks]
    value_specs = [pl.BlockSpec((c.shape[0], pair), lambda j: (0, j + pairs)) for c in kv_chunks]
    row_spec = pl.BlockSpec((token_count, pair), lambda j: (0, j))
    stat_width = 128
    if whole_output:
        out_specs = [
            pl.BlockSpec(memory_space=pltpu.VMEM),
            pl.BlockSpec(memory_space=pltpu.VMEM),
        ]
    else:
        out_specs = [row_spec, pl.BlockSpec((token_count, stat_width), lambda j: (0, 0))]
    extra = [] if after is None else [after]
    extra_specs = [pl.BlockSpec(memory_space=pl.ANY) for _ in extra]
    keys = sum(c.shape[0] for c in kv_chunks)
    cost = pl.CostEstimate(
        flops=8 * token_count * keys * model_width,
        transcendentals=token_count * keys * (model_width // head_size),
        bytes_accessed=2 * keys * 2 * model_width + 8 * token_count * model_width,
    )
    heads = model_width // head_size
    stat_rows = -(-heads // 8) * 8
    if rows_out:
        out_specs = out_specs + [pl.BlockSpec((stat_rows, stat_width), lambda j: (0, 0))]
    out_shape = [
        jax.ShapeDtypeStruct((token_count, model_width), out_dtype),
        jax.ShapeDtypeStruct((token_count, stat_width), jnp.float32),
    ]
    if rows_out:
        out_shape.append(jax.ShapeDtypeStruct((stat_rows, stat_width), jnp.float32))
    results = pl.pallas_call(
        kernel,
        grid=(pairs,),
        cost_estimate=cost,
        in_specs=[row_spec] + key_specs + value_specs + extra_specs,
        out_specs=out_specs,
        out_shape=out_shape,
    )(queries, *kv_chunks, *kv_chunks, *extra)
    if rows_out:
        return results[0], results[2]
    return results[0], results[1]


def exchanged(x, mask):
    devices = lax.axis_size("seq")
    return lax.ppermute(x, "seq", [(i, i ^ mask) for i in range(devices)])


def projected(rows, norm_gain, weight):
    normed = layer_norm(rows, norm_gain).astype(jnp.bfloat16)
    return jnp.dot(normed, weight, preferred_element_type=jnp.float32).astype(jnp.bfloat16)


def body(layer_input, norm_gain, projection, output_weight, deep_weight, skip_weight, conv_kernel):
    token_count, model_width = layer_input.shape
    head_size = model_width // HEADS
    score_scale = 1.0 / math.sqrt(head_size)
    half = lax.axis_size("seq") // 2
    queries = projected(layer_input, norm_gain, projection[:, :model_width])
    mirrored_queries = exchanged(queries, half)
    same_core = [layer_input] + [exchanged(layer_input, mask) for mask in range(2, half, 2)]
    mine = jnp.concatenate(same_core, axis=0)
    theirs = exchanged(mine, 1)
    kv_weight = projection[:, model_width:]
    kv_chunks = [projected(mine, norm_gain, kv_weight), projected(theirs, norm_gain, kv_weight)]
    remote_out, remote_lse = attention(
        mirrored_queries, kv_chunks, head_size, score_scale, jnp.bfloat16, False, rows_out=True
    )
    heads = model_width // head_size
    other_out = exchanged(remote_out, half)
    row_major = Layout(major_to_minor=(0, 1))
    sent_lse = with_layout_constraint(remote_lse, row_major)
    other_lse = with_layout_constraint(exchanged(sent_lse, half), row_major)[:heads].T
    own_out, own_lse = attention(
        queries, kv_chunks, head_size, score_scale, jnp.float32, False
    )
    own_lse = own_lse[:, :heads]
    top = jnp.maximum(own_lse, other_lse) + 0 * other_out[:1, :1].astype(jnp.float32)
    own_weight = jnp.repeat(jnp.exp(own_lse - top), head_size, axis=1)
    other_weight = jnp.repeat(jnp.exp(other_lse - top), head_size, axis=1)
    attended = (
        (own_weight * own_out + other_weight * other_out.astype(jnp.float32))
        / (own_weight + other_weight)
    ).astype(jnp.bfloat16)
    encoded = (
        layer_input.astype(jnp.float32)
        + jnp.dot(attended, output_weight, preferred_element_type=jnp.float32)
    ).astype(jnp.bfloat16)
    position = lax.axis_index("seq")
    half_rows = token_count // GZ
    input_grid = layer_input.reshape(1, half_rows, GZ, model_width)
    encoded_grid = encoded.reshape(1, half_rows, GZ, model_width)
    joined = jnp.concatenate(
        [upsample(encoded_grid, deep_weight), upsample(input_grid, skip_weight)], axis=-1
    )
    lower_half = position % 2 == 0
    boundary = jnp.where(lower_half, joined[:, -1:], joined[:, :1])
    partner = swapped(boundary, "seq", 0)
    zero_plane = jnp.zeros_like(partner)
    low_rim = jnp.where(lower_half, zero_plane, partner)
    high_rim = jnp.where(lower_half, partner, zero_plane)
    extended = jnp.concatenate([low_rim, joined, high_rim], axis=1)
    low_plane = plane_send(extended[-1:], 2)
    high_plane = plane_send(extended[:1], -2)
    decoded = convolve(extended, low_plane, high_plane, conv_kernel)[None]
    return (encoded, decoded)


def solution(mesh):
    return jax.shard_map(
        body,
        mesh=mesh,
        in_specs=(P(("groups", "seq"), None), P(), P(), P(), P(), P(), P()),
        out_specs=(P(("groups", "seq"), None), P(("groups", "seq"), None, None, None, None)),
        check_vma=False,
    )
```

```python
import math

import jax
import jax.numpy as jnp
from jax import lax
from jax.experimental import pallas as pl
from jax.experimental.pallas import tpu as pltpu
from jax.experimental.layout import Layout, with_layout_constraint
from jax.sharding import PartitionSpec as P

HEADS = 12
GZ = 8


epsilon = 1e-06
leak_slope = 0.01


def shifted(block, axis, distance):
    devices = range(lax.axis_size(axis))
    route = [(i - distance, i) for i in devices if i - distance in devices]
    return lax.ppermute(block, axis, route)


def swapped(x, axis, distance):
    return lax.ppermute(x, axis, [(i, i ^ 1 << distance) for i in range(lax.axis_size(axis))])


def layer_norm(inputs, gain):
    values32 = inputs.astype(jnp.float32)
    row_mean = jnp.mean(values32, axis=-1, keepdims=True)
    centered = values32 - row_mean
    row_var = jnp.mean(centered * centered, axis=-1, keepdims=True)
    return centered * lax.rsqrt(row_var + epsilon) * gain.astype(jnp.float32)


def to_voxels(flat_out, channels):
    extent_x, extent_y, extent_z = (flat_out.shape[0], flat_out.shape[1], flat_out.shape[2])
    shaped = flat_out.reshape(extent_x, extent_y, extent_z, 2, 2, 2, channels)
    shaped = shaped.transpose(0, 3, 1, 4, 2, 5, 6)
    return shaped.reshape(2 * extent_x, 2 * extent_y, 2 * extent_z, channels)


def upsample(token_grid, weight):
    model_width = token_grid.shape[-1]
    product = jnp.dot(
        token_grid.reshape(-1, model_width), weight, preferred_element_type=jnp.float32
    )
    flat_out = product.astype(jnp.bfloat16).reshape(token_grid.shape[:3] + (weight.shape[1],))
    return to_voxels(flat_out, weight.shape[1] // 8)


def convolve(extended, low_plane, high_plane, conv_kernel):
    def conv(field, kernel, x_pad):
        return lax.conv_general_dilated(
            field.transpose(0, 2, 1, 3)[None],
            kernel.transpose(0, 2, 1, 3, 4),
            window_strides=(1, 1, 1),
            padding=((x_pad, x_pad), (1, 1), (0, 0)),
            dimension_numbers=("NDHWC", "DHWIO", "NDHWC"),
            preferred_element_type=jnp.float32,
        )[0].transpose(0, 2, 1, 3)

    interior = lax.optimization_barrier(conv(extended, conv_kernel, 1))
    rims = jnp.concatenate(
        [conv(low_plane, conv_kernel[:1], 0), conv(high_plane, conv_kernel[2:], 0)], axis=0
    )
    accumulated = interior + rims
    activated = jnp.where(accumulated > 0, accumulated, leak_slope * accumulated)
    return activated.astype(jnp.bfloat16)


def plane_send(plane, offset):
    return shifted(plane, "seq", offset)


def attention_kernel(*refs, head_size, score_scale, chunks, whole_output, ordered, rows_out):
    rows_ref = None
    if rows_out:
        rows_ref = refs[-1]
        refs = refs[:-1]
    if ordered:
        refs = refs[:-3] + refs[-2:]
    q_ref = refs[0]
    k_refs = refs[1 : 1 + chunks]
    v_refs = refs[1 + chunks : 1 + 2 * chunks]
    o_ref, lse_ref = refs[-2:]
    step = pl.program_id(0)
    pair = q_ref.shape[-1]
    lane = lax.broadcasted_iota(jnp.int32, (1, pair), 1)
    stat_lane = lax.broadcasted_iota(jnp.int32, (1, lse_ref.shape[-1]), 1)

    @pl.when(step == 0)
    def _():
        lse_ref[...] = jnp.zeros_like(lse_ref)

    q = q_ref[...]
    result = None
    log_sum = lse_ref[...]
    heads = pair // head_size
    for h in range(heads):
        in_head = (lane >= h * head_size) & (lane < (h + 1) * head_size)
        q_h = jnp.where(in_head, q, jnp.zeros_like(q))
        scores = [
            lax.dot_general(
                q_h, k_ref[...], (((1,), (1,)), ((), ())), preferred_element_type=jnp.float32
            )
            for k_ref in k_refs
        ]
        raw_max = scores[0].max(axis=-1, keepdims=True)
        for block in scores[1:]:
            raw_max = jnp.maximum(raw_max, block.max(axis=-1, keepdims=True))
        row_max = raw_max * score_scale
        denominator = None
        numerator = None
        for block, v_ref in zip(scores, v_refs):
            exp_scores = jnp.exp2((block - raw_max) * (score_scale * math.log2(math.e)))
            part_sum = jnp.sum(exp_scores, axis=-1, keepdims=True)
            part = jnp.dot(
                exp_scores.astype(jnp.bfloat16), v_ref[...], preferred_element_type=jnp.float32
            )
            denominator = part_sum if denominator is None else denominator + part_sum
            numerator = part if numerator is None else numerator + part
        head_out = numerator / denominator
        head_lse = row_max + jnp.log(denominator)
        result = head_out if result is None else jnp.where(in_head, head_out, result)
        log_sum = jnp.where(stat_lane == step * heads + h, head_lse, log_sum)
    if whole_output:
        o_ref[:, pl.ds(pl.multiple_of(step * pair, pair), pair)] = result.astype(o_ref.dtype)
    else:
        o_ref[...] = result.astype(o_ref.dtype)
    lse_ref[...] = log_sum
    if rows_out:

        @pl.when(step == pl.num_programs(0) - 1)
        def _():
            rows_ref[...] = jnp.transpose(log_sum)[: rows_ref.shape[0]]


def attention(
    queries, kv_chunks, head_size, score_scale, out_dtype, whole_output, after=None, rows_out=False
):
    token_count, model_width = queries.shape
    pair = 2 * head_size
    pairs = model_width // pair
    chunks = len(kv_chunks)
    kernel = lambda *refs: attention_kernel(
        *refs,
        head_size=head_size,
        score_scale=score_scale,
        chunks=chunks,
        whole_output=whole_output,
        ordered=after is not None,
        rows_out=rows_out,
    )
    key_specs = [pl.BlockSpec((c.shape[0], pair), lambda j: (0, j)) for c in kv_chunks]
    value_specs = [pl.BlockSpec((c.shape[0], pair), lambda j: (0, j + pairs)) for c in kv_chunks]
    row_spec = pl.BlockSpec((token_count, pair), lambda j: (0, j))
    stat_width = 128
    if whole_output:
        out_specs = [
            pl.BlockSpec(memory_space=pltpu.VMEM),
            pl.BlockSpec(memory_space=pltpu.VMEM),
        ]
    else:
        out_specs = [row_spec, pl.BlockSpec((token_count, stat_width), lambda j: (0, 0))]
    extra = [] if after is None else [after]
    extra_specs = [pl.BlockSpec(memory_space=pl.ANY) for _ in extra]
    keys = sum(c.shape[0] for c in kv_chunks)
    cost = pl.CostEstimate(
        flops=8 * token_count * keys * model_width,
        transcendentals=token_count * keys * (model_width // head_size),
        bytes_accessed=2 * keys * 2 * model_width + 8 * token_count * model_width,
    )
    heads = model_width // head_size
    stat_rows = -(-heads // 8) * 8
    if rows_out:
        out_specs = out_specs + [pl.BlockSpec((stat_rows, stat_width), lambda j: (0, 0))]
    out_shape = [
        jax.ShapeDtypeStruct((token_count, model_width), out_dtype),
        jax.ShapeDtypeStruct((token_count, stat_width), jnp.float32),
    ]
    if rows_out:
        out_shape.append(jax.ShapeDtypeStruct((stat_rows, stat_width), jnp.float32))
    results = pl.pallas_call(
        kernel,
        grid=(pairs,),
        cost_estimate=cost,
        in_specs=[row_spec] + key_specs + value_specs + extra_specs,
        out_specs=out_specs,
        out_shape=out_shape,
    )(queries, *kv_chunks, *kv_chunks, *extra)
    if rows_out:
        return results[0], results[2]
    return results[0], results[1]


def exchanged(x, mask):
    devices = lax.axis_size("seq")
    return lax.ppermute(x, "seq", [(i, i ^ mask) for i in range(devices)])


def projected(rows, norm_gain, weight):
    normed = layer_norm(rows, norm_gain).astype(jnp.bfloat16)
    return jnp.dot(normed, weight, preferred_element_type=jnp.float32).astype(jnp.bfloat16)


def body(layer_input, norm_gain, projection, output_weight, deep_weight, skip_weight, conv_kernel):
    token_count, model_width = layer_input.shape
    head_size = model_width // HEADS
    score_scale = 1.0 / math.sqrt(head_size)
    half = lax.axis_size("seq") // 2
    queries = projected(layer_input, norm_gain, projection[:, :model_width])
    mirrored_queries = exchanged(queries, half)
    same_core = [layer_input] + [exchanged(layer_input, mask) for mask in range(2, half, 2)]
    mine = jnp.concatenate(same_core, axis=0)
    theirs = exchanged(mine, 1)
    mirrored_queries, theirs = lax.optimization_barrier((mirrored_queries, theirs))
    kv_weight = projection[:, model_width:]
    kv_chunks = [projected(mine, norm_gain, kv_weight), projected(theirs, norm_gain, kv_weight)]
    remote_out, remote_lse = attention(
        mirrored_queries, kv_chunks, head_size, score_scale, jnp.bfloat16, False, rows_out=True
    )
    heads = model_width // head_size
    other_out = exchanged(remote_out, half)
    row_major = Layout(major_to_minor=(0, 1))
    sent_lse = with_layout_constraint(remote_lse, row_major)
    other_lse = with_layout_constraint(exchanged(sent_lse, half), row_major)[:heads].T
    own_out, own_lse = attention(
        queries, kv_chunks, head_size, score_scale, jnp.float32, False
    )
    own_lse = own_lse[:, :heads]
    top = jnp.maximum(own_lse, other_lse) + 0 * other_out[:1, :1].astype(jnp.float32)
    own_weight = jnp.repeat(jnp.exp(own_lse - top), head_size, axis=1)
    other_weight = jnp.repeat(jnp.exp(other_lse - top), head_size, axis=1)
    attended = (
        (own_weight * own_out + other_weight * other_out.astype(jnp.float32))
        / (own_weight + other_weight)
    ).astype(jnp.bfloat16)
    encoded = (
        layer_input.astype(jnp.float32)
        + jnp.dot(attended, output_weight, preferred_element_type=jnp.float32)
    ).astype(jnp.bfloat16)
    position = lax.axis_index("seq")
    half_rows = token_count // GZ
    input_grid = layer_input.reshape(1, half_rows, GZ, model_width)
    encoded_grid = encoded.reshape(1, half_rows, GZ, model_width)
    joined = jnp.concatenate(
        [upsample(encoded_grid, deep_weight), upsample(input_grid, skip_weight)], axis=-1
    )
    lower_half = position % 2 == 0
    boundary = jnp.where(lower_half, joined[:, -1:], joined[:, :1])
    partner = swapped(boundary, "seq", 0)
    zero_plane = jnp.zeros_like(partner)
    low_rim = jnp.where(lower_half, zero_plane, partner)
    high_rim = jnp.where(lower_half, partner, zero_plane)
    extended = jnp.concatenate([low_rim, joined, high_rim], axis=1)
    low_plane = plane_send(extended[-1:], 2)
    high_plane = plane_send(extended[:1], -2)
    decoded = convolve(extended, low_plane, high_plane, conv_kernel)[None]
    return (encoded, decoded)


def solution(mesh):
    return jax.shard_map(
        body,
        mesh=mesh,
        in_specs=(P(("groups", "seq"), None), P(), P(), P(), P(), P(), P()),
        out_specs=(P(("groups", "seq"), None), P(("groups", "seq"), None, None, None, None)),
        check_vma=False,
    )
```
